32 devices in a mesh: grp: 2 (over y), ctx: 4 (over z), tp: 4 (over x, core).
Axes of the slice: x: 2, y: 2, z: 4, core: 2. Of those that a mesh axis runs over, the one named last changes fastest.
Arguments:
- tokens: bfloat16 [3072, 4096], P(('grp', 'ctx'), 'tp'), parts along dimension 0, may hold values from -6 to 6
- norm_gain: bfloat16 [4096], P('tp'), may hold values from 0.099609375 to 1.8984375
- w_in: bfloat16 [4096, 3, 2048], P('ctx', None, 'tp'), may hold values from -0.09375 to 0.09375
- short_taps: float32 [3, 3, 2048], P(None, None, 'tp'), may hold values from -3.5 to 3.5
- rates: float32 [128, 64], P('tp'), may hold values from 6.510417e-06 to 0.03
- residues: float32 [128, 64], P('tp'), may hold values from -4 to 4
- w_out: bfloat16 [2048, 4096], P(None, 'tp'), may hold values from -0.125 to 0.125
Outputs:
- layer_out: bfloat16 [3072, 4096], P(('grp', 'ctx'), 'tp'), parts along dimension 0
The draws below stay inside these ranges and needn't reach their ends.
There are 2 independent parts, one for each index of `grp`. The reference program is written for one: setup_inputs(seed, part) draws one part's arguments, and reference() takes and returns one part's arrays. A program takes and returns all parts, laid end to end along the dimension named above; an argument that names none is the same for every part. Nothing has to cross between parts.
All inputs are finite; a program needn't handle non-finite values.
Results may differ from the reference program's by a relative error of at most 0.0067.
Values may be sent and summed in bfloat16 or wider, within the bound.
No kernel may reach another device: no remote copies, remote signals or barrier semaphores. Data moves between devices by JAX's collectives and lax.ppermute only.
A program may use at most 128 MiB of HBM per device.

```python
import math
import jax
import jax.numpy as jnp
from jax import lax

D = 4096
C = 2048
GROUP = 16
SHORT = 3
MODES = 64
SEQ = 1536
GROUPS = 128


def draw_rates(key, part):
    low_log = math.log(0.01 / SEQ)
    high_log = math.log(0.03)
    first_key = jax.random.fold_in(key, 0)
    uniform_all = jax.random.uniform(first_key, (GROUPS, MODES), jnp.float32)
    log_rates = low_log + (high_log - low_log) * uniform_all
    return jnp.exp(log_rates).astype(jnp.float32)


def steps_of(rng, shape, cuts, least, high):
    def one(dim, shards_of):
        steps = jax.random.uniform(jax.random.fold_in(jax.random.fold_in(rng, 6), dim), (shards_of,), jnp.float32, least / len(cuts), high / len(cuts))
        return jnp.repeat(jnp.exp(steps), shape[dim] // shards_of).reshape((-1,) + (1,) * (len(shape) - dim - 1))

    loudness = one(*cuts[0])
    for cut in cuts[1:]:
        loudness = loudness * one(*cut)
    return loudness


def bell_draw(stream_key, shape, deviation, bound, shards=(), dtype=jnp.bfloat16):
    array = jax.random.normal(stream_key, shape, jnp.float32) * deviation
    if len(shards) > 0:
        array = steps_of(stream_key, shape, shards, -0.22, 0.18) * array
    return jnp.clip(array, min=-bound, max=bound).astype(dtype)


def setup_inputs(seed: int = 0, part: int = 0) -> dict:
    arg_keys = jax.random.split(jax.random.key(seed), 8)
    own_keys = jax.random.split(jax.random.fold_in(arg_keys[7], part), 8)
    tokens = bell_draw(own_keys[0], (SEQ, D), 1.0, 6.0, ((0, 4), (1, 4)))
    norm_gain = jnp.clip(1.0 + 0.18 * jax.random.normal(arg_keys[1], (D,), jnp.float32), 0.099609375, 1.8984375).astype(jnp.bfloat16)
    w_in = bell_draw(arg_keys[2], (D, 3, C), D ** -0.5, 0.09375, ((0, 4), (2, 4)))
    short_taps = bell_draw(arg_keys[3], (SHORT, 3, C), SHORT ** -0.5, 3.5, ((2, 4),), jnp.float32)
    rates = draw_rates(jax.random.fold_in(arg_keys[7], 71), part)
    residues = bell_draw(arg_keys[5], (GROUPS, MODES), 1.0, 4.0, ((0, 4),), jnp.float32)
    w_out = bell_draw(arg_keys[6], (C, D), C ** -0.5, 0.125, ((1, 4),))
    return dict(tokens=tokens, norm_gain=norm_gain, w_in=w_in, short_taps=short_taps, rates=rates, residues=residues, w_out=w_out)


def long_response(rates, residues, length):
    coef = residues * jnp.sqrt(-jnp.expm1(-2.0 * rates)) * MODES ** (-0.5)
    lags = jnp.arange(length).astype(jnp.float32)

    def one_group(pair):
        group_rates, group_coef = pair
        powers = jnp.exp(-group_rates[:, None] * lags[None, :])
        return jnp.dot(group_coef, powers, precision=lax.Precision.HIGHEST)
    return lax.map(one_group, (rates, coef))

def reference(tokens, norm_gain, w_in, short_taps, rates, residues, w_out):
    values = tokens.astype(jnp.float32)
    scale = lax.rsqrt(lax.optimization_barrier(jnp.mean(values * values, axis=1, keepdims=True)) + 1e-06)
    normed = (values * scale * norm_gain.astype(jnp.float32)).astype(jnp.bfloat16)
    projected = jnp.dot(normed, w_in.reshape(D, 3 * C), preferred_element_type=jnp.float32).astype(jnp.bfloat16)
    padded = jnp.pad(projected.astype(jnp.float32), ((SHORT - 1, 0), (0, 0)))
    taps = short_taps.reshape(SHORT, 3 * C)
    filtered = jnp.zeros((SEQ, 3 * C), jnp.float32)
    for tap_index in range(SHORT):
        begin = SHORT - 1 - tap_index
        filtered = filtered + taps[tap_index] * padded[begin:begin + SEQ]
    product = filtered[:, :C] * filtered[:, 2 * C:]
    second = filtered[:, C:2 * C]
    response = long_response(rates, residues, SEQ)
    grouped = product.reshape(SEQ, GROUPS, GROUP).transpose(1, 0, 2)
    doubled = 2 * SEQ

    def convolve(pair):
        group_taps, channel_block = pair
        spectrum = jnp.fft.rfft(group_taps, n=doubled)[:, None] * jnp.fft.rfft(channel_block, n=doubled, axis=0)
        return jnp.fft.irfft(spectrum, n=doubled, axis=0)[:SEQ]
    convolved = lax.map(convolve, (response, grouped))
    conv_out = convolved.transpose(1, 0, 2).reshape(SEQ, C).astype(jnp.float32)
    gated = (second * conv_out).astype(jnp.bfloat16)
    return (values + jnp.dot(gated, w_out, preferred_element_type=jnp.float32)).astype(jnp.bfloat16)
```

```python
import jax
import jax.numpy as jnp
from jax import lax
from jax.sharding import PartitionSpec as P

BLOCK = 128


def shifted(x, axis, by):
    count = lax.axis_size(axis)
    pairs = [(i, i + by) for i in range(count) if 0 <= i + by < count]
    return lax.ppermute(x, axis, pairs)


def short_filter(extended, taps, count):
    values = extended.astype(jnp.float32)
    result = jnp.zeros((count, values.shape[1]), jnp.float32)
    span = taps.shape[0]
    for tap_index in range(span):
        begin = span - 1 - tap_index
        result = result + taps[tap_index] * values[begin : begin + count]
    return result


def banded(series):
    group_count, length = series.shape
    padded = jnp.concatenate([series, jnp.zeros_like(series)], axis=1)
    tiled = jnp.tile(padded, (1, length))
    return tiled[:, : length * (2 * length - 1)].reshape(group_count, length, 2 * length - 1)


def gather_by_permutes(x, axis):
    count = lax.axis_size(axis)
    me = lax.axis_index(axis)
    pieces = [x]
    for by in range(1, count):
        pairs = [(s, (s + by) % count) for s in range(count)]
        pieces.append(lax.ppermute(x, axis, pairs))
    stacked = jnp.stack(pieces[::-1], axis=0)
    return jnp.roll(stacked, me + 1, axis=0)


def body(tokens, norm_gain, w_in, short_taps, rates, residues, w_out):
    tok_rows = tokens.shape[0]
    local_width = w_in.shape[2]
    local_groups = rates.shape[0]
    group_size = local_width // local_groups
    block_rows = BLOCK
    reach = block_rows - 1
    mode_count = rates.shape[1]
    highest = lax.Precision.HIGHEST
    n_ctx = lax.axis_size("ctx")
    n_grp = lax.axis_size("grp")
    me_ctx = lax.axis_index("ctx")
    me_grp = lax.axis_index("grp")
    shard_rows = w_in.shape[0]
    piece = shard_rows // n_grp
    streams = w_in.shape[1]

    own = lax.dynamic_slice_in_dim(w_in, me_grp * piece, piece, axis=0)
    relayed = []
    for s in range(streams):
        got = lax.all_gather(own[:, s, :], "ctx", axis=0)
        doubled = jnp.concatenate([got, got], axis=0)
        send = lax.dynamic_slice_in_dim(doubled, me_ctx + 1, n_ctx - 1, axis=0)
        received = []
        for by in range(1, n_grp):
            pairs = [(q, (q + by) % n_grp) for q in range(n_grp)]
            received.append(lax.ppermute(send, "grp", pairs))
        relayed.append((got, received))

    with_gain = jnp.concatenate([tokens, norm_gain[None]], axis=0)
    stacked = gather_by_permutes(with_gain, "tp")
    gathered = jnp.concatenate(list(stacked), axis=1)
    values = gathered[:tok_rows].astype(jnp.float32)
    gain_whole = gathered[tok_rows]
    scale = lax.rsqrt(jnp.mean(values * values, axis=1, keepdims=True) + 1e-06)
    normed = (values * scale * gain_whole.astype(jnp.float32)).astype(jnp.bfloat16)
    normed4 = normed.reshape(tok_rows, n_ctx, n_grp, piece)
    mine = lax.dynamic_index_in_dim(normed4, me_grp, axis=2, keepdims=False)
    others = []
    for by in range(1, n_grp):
        src_grp = (me_grp - by) % n_grp
        part = lax.dynamic_index_in_dim(normed4, src_grp, axis=2, keepdims=False)
        others.append((src_grp, jnp.roll(part, -me_ctx, axis=1)))
    outputs = []
    for s in range(streams):
        got, received = relayed[s]
        acc = jnp.einsum("tkr,krc->tc", mine, got, preferred_element_type=jnp.float32)
        for (src_grp, part), recv in zip(others, received):
            local = lax.dynamic_slice_in_dim(w_in[:, s, :], src_grp * piece, piece, axis=0)
            acc = acc + jnp.dot(part[:, 0], local, preferred_element_type=jnp.float32)
            acc = acc + jnp.einsum(
                "tkr,krc->tc", part[:, 1:], recv, preferred_element_type=jnp.float32
            )
        outputs.append(acc)
    projected = jnp.concatenate(outputs, axis=1).astype(jnp.bfloat16)
    span = short_taps.shape[0]
    taps = short_taps.reshape(span, 3 * local_width)
    before = shifted(projected[tok_rows - (span - 1) :], "ctx", 1)
    filtered = short_filter(jnp.concatenate([before, projected], axis=0), taps, tok_rows)
    product = filtered[:, :local_width] * filtered[:, 2 * local_width :]
    second = filtered[:, local_width : 2 * local_width]
    decay = rates[:, :, None]
    coef = residues * jnp.sqrt(-jnp.expm1(-2.0 * rates)) * mode_count ** (-0.5)
    lags = jnp.arange(block_rows).astype(jnp.float32)
    powers = jnp.exp(-decay * lags)
    long_taps = jnp.einsum("gn,gnt->gt", coef, powers, precision=highest)
    kernel = banded(long_taps[:, ::-1])[:, :, reach:]
    blocks = tok_rows // block_rows
    current = product.reshape(blocks, block_rows, local_groups, group_size)
    near = jnp.einsum("gij,bjgc->bigc", kernel, current, precision=highest)
    tail = jnp.exp(-decay * (reach - lags))
    ends = jnp.einsum("gni,bigc->bgnc", tail, current, precision=highest)
    step_decay = jnp.exp(-decay * block_rows)

    def advance(state, end_block):
        return (step_decay * state + end_block, state)

    zero_state = jnp.zeros((local_groups, mode_count, group_size), jnp.float32)
    own_state, local_starts = lax.scan(advance, zero_state, ends)
    position = lax.axis_index("ctx")
    shards = lax.all_gather(own_state[None], "ctx", axis=0, tiled=True)
    source = jnp.arange(shards.shape[0])
    distance = (position - 1 - source).astype(jnp.float32)[:, None, None]
    weight = jnp.where(
        distance >= 0.0, jnp.exp(-rates[None] * tok_rows * jnp.maximum(distance, 0.0)), 0.0
    )
    incoming = jnp.einsum("kgn,kgnc->gnc", weight, shards, precision=highest)
    block_index = jnp.arange(blocks).astype(jnp.float32)
    lead = jnp.exp(-decay[None] * block_rows * block_index[:, None, None, None])
    starts = lead * incoming[None] + local_starts
    entry = coef[:, None, :] * jnp.exp(-rates[:, None, :] * (lags[None, :, None] + 1.0))
    distant = jnp.einsum("gin,bgnc->bigc", entry, starts, precision=highest)
    conv_out = (near + distant).reshape(tok_rows, local_width)
    gated = (second * conv_out).astype(jnp.bfloat16)
    mixed = jnp.dot(
        lax.all_gather(gated, "tp", axis=1, tiled=True), w_out, preferred_element_type=jnp.float32
    )
    return (tokens.astype(jnp.float32) + mixed).astype(jnp.bfloat16)


def solution(mesh):
    in_specs = (
        P(("grp", "ctx"), "tp"),
        P("tp"),
        P("ctx", None, "tp"),
        P(None, None, "tp"),
        P("tp", None),
        P("tp", None),
        P(None, "tp"),
    )
    out_specs = P(("grp", "ctx"), "tp")
    return jax.shard_map(body, mesh=mesh, in_specs=in_specs, out_specs=out_specs, check_vma=False)
```

```python
import jax
import jax.numpy as jnp
from jax import lax
from jax.sharding import PartitionSpec as P

BLOCK = 128


def shifted(x, axis, by):
    count = lax.axis_size(axis)
    pairs = [(i, i + by) for i in range(count) if 0 <= i + by < count]
    return lax.ppermute(x, axis, pairs)


def short_filter(extended, taps, count):
    values = extended.astype(jnp.float32)
    result = jnp.zeros((count, values.shape[1]), jnp.float32)
    span = taps.shape[0]
    for tap_index in range(span):
        begin = span - 1 - tap_index
        result = result + taps[tap_index] * values[begin : begin + count]
    return result


def banded(series):
    group_count, length = series.shape
    padded = jnp.concatenate([series, jnp.zeros_like(series)], axis=1)
    tiled = jnp.tile(padded, (1, length))
    return tiled[:, : length * (2 * length - 1)].reshape(group_count, length, 2 * length - 1)


def gather_by_permutes(x, axis):
    count = lax.axis_size(axis)
    me = lax.axis_index(axis)
    pieces = [x]
    for by in range(1, count):
        pairs = [(s, (s + by) % count) for s in range(count)]
        pieces.append(lax.ppermute(x, axis, pairs))
    stacked = jnp.stack(pieces[::-1], axis=0)
    return jnp.roll(stacked, me + 1, axis=0)


def body(tokens, norm_gain, w_in, short_taps, rates, residues, w_out):
    tok_rows = tokens.shape[0]
    local_width = w_in.shape[2]
    local_groups = rates.shape[0]
    group_size = local_width // local_groups
    block_rows = BLOCK
    reach = block_rows - 1
    mode_count = rates.shape[1]
    highest = lax.Precision.HIGHEST
    n_ctx = lax.axis_size("ctx")
    n_grp = lax.axis_size("grp")
    me_ctx = lax.axis_index("ctx")
    me_grp = lax.axis_index("grp")
    shard_rows = w_in.shape[0]
    piece = shard_rows // n_grp
    streams = w_in.shape[1]

    span = short_taps.shape[0]
    halo = span - 1
    decay = rates[:, :, None]
    coef = residues * jnp.sqrt(-jnp.expm1(-2.0 * rates)) * mode_count ** (-0.5)
    lags = jnp.arange(block_rows).astype(jnp.float32)
    powers = jnp.exp(-decay * lags)
    long_taps = jnp.einsum("gn,gnt->gt", coef, powers, precision=highest)
    kernel = banded(long_taps[:, ::-1])[:, :, reach:]
    tail = jnp.exp(-decay * (reach - lags))
    entry = coef[:, None, :] * jnp.exp(-rates[:, None, :] * (lags[None, :, None] + 1.0))

    own = lax.dynamic_slice_in_dim(w_in, me_grp * piece, piece, axis=0)
    relayed = []
    for s in range(streams):
        got = lax.all_gather(own[:, s, :], "ctx", axis=0)
        if s == 0:
            got, kernel, tail, entry = lax.optimization_barrier((got, kernel, tail, entry))
        doubled = jnp.concatenate([got, got], axis=0)
        send = lax.dynamic_slice_in_dim(doubled, me_ctx + 1, n_ctx - 1, axis=0)
        received = []
        for by in range(1, n_grp):
            pairs = [(q, (q + by) % n_grp) for q in range(n_grp)]
            received.append(lax.ppermute(send, "grp", pairs))
        relayed.append((got, received))

    before = shifted(tokens[tok_rows - halo :], "ctx", 1)
    with_gain = jnp.concatenate([before, tokens, norm_gain[None]], axis=0)
    stacked = gather_by_permutes(with_gain, "tp")
    gathered = jnp.concatenate(list(stacked), axis=1)
    ext_rows = tok_rows + halo
    values = gathered[:ext_rows].astype(jnp.float32)
    gain_whole = gathered[ext_rows]
    scale = lax.rsqrt(jnp.mean(values * values, axis=1, keepdims=True) + 1e-06)
    normed = (values * scale * gain_whole.astype(jnp.float32)).astype(jnp.bfloat16)
    normed4 = normed.reshape(ext_rows, n_ctx, n_grp, piece)
    mine = lax.dynamic_index_in_dim(normed4, me_grp, axis=2, keepdims=False)
    others = []
    for by in range(1, n_grp):
        src_grp = (me_grp - by) % n_grp
        part = lax.dynamic_index_in_dim(normed4, src_grp, axis=2, keepdims=False)
        others.append((src_grp, jnp.roll(part, -me_ctx, axis=1)))
    outputs = []
    for s in range(streams):
        got, received = relayed[s]
        acc = jnp.einsum("tkr,krc->tc", mine, got, preferred_element_type=jnp.float32)
        for (src_grp, part), recv in zip(others, received):
            local = lax.dynamic_slice_in_dim(w_in[:, s, :], src_grp * piece, piece, axis=0)
            acc = acc + jnp.dot(part[:, 0], local, preferred_element_type=jnp.float32)
            acc = acc + jnp.einsum(
                "tkr,krc->tc", part[:, 1:], recv, preferred_element_type=jnp.float32
            )
        outputs.append(acc)
    extended = jnp.concatenate(outputs, axis=1).astype(jnp.bfloat16)
    taps = short_taps.reshape(span, 3 * local_width)
    filtered = short_filter(extended, taps, tok_rows)
    product = filtered[:, :local_width] * filtered[:, 2 * local_width :]
    second = filtered[:, local_width : 2 * local_width]
    blocks = tok_rows // block_rows
    current = product.reshape(blocks, block_rows, local_groups, group_size)
    near = jnp.einsum("gij,bjgc->bigc", kernel, current, precision=highest)
    ends = jnp.einsum("gni,bigc->bgnc", tail, current, precision=highest)
    step_decay = jnp.exp(-decay * block_rows)

    def advance(state, end_block):
        return (step_decay * state + end_block, state)

    zero_state = jnp.zeros((local_groups, mode_count, group_size), jnp.float32)
    own_state, local_starts = lax.scan(advance, zero_state, ends)
    incoming = jnp.zeros_like(own_state)
    for by in range(1, n_ctx):
        pairs = [(k, k + by) for k in range(n_ctx - by)]
        arrived = lax.ppermute(own_state, "ctx", pairs)
        incoming = incoming + jnp.exp(-decay * (tok_rows * (by - 1.0))) * arrived
    block_index = jnp.arange(blocks).astype(jnp.float32)
    lead = jnp.exp(-decay[None] * block_rows * block_index[:, None, None, None])
    starts = lead * incoming[None] + local_starts
    distant = jnp.einsum("gin,bgnc->bigc", entry, starts, precision=highest)
    conv_out = (near + distant).reshape(tok_rows, local_width)
    gated = (second * conv_out).astype(jnp.bfloat16)
    mixed = jnp.dot(
        lax.all_gather(gated, "tp", axis=1, tiled=True), w_out, preferred_element_type=jnp.float32
    )
    return (tokens.astype(jnp.float32) + mixed).astype(jnp.bfloat16)


def solution(mesh):
    in_specs = (
        P(("grp", "ctx"), "tp"),
        P("tp"),
        P("ctx", None, "tp"),
        P(None, None, "tp"),
        P("tp", None),
        P("tp", None),
        P(None, "tp"),
    )
    out_specs = P(("grp", "ctx"), "tp")
    return jax.shard_map(body, mesh=mesh, in_specs=in_specs, out_specs=out_specs, check_vma=False)
```

```python
import jax
import jax.numpy as jnp
from jax import lax
from jax.sharding import PartitionSpec as P

BLOCK = 128


def shifted(x, axis, by):
    count = lax.axis_size(axis)
    pairs = [(i, i + by) for i in range(count) if 0 <= i + by < count]
    return lax.ppermute(x, axis, pairs)


def short_filter(extended, taps, count):
    values = extended.astype(jnp.float32)
    result = jnp.zeros((count, values.shape[1]), jnp.float32)
    span = taps.shape[0]
    for tap_index in range(span):
        begin = span - 1 - tap_index
        result = result + taps[tap_index] * values[begin : begin + count]
    return result


def banded(series):
    group_count, length = series.shape
    padded = jnp.concatenate([series, jnp.zeros_like(series)], axis=1)
    tiled = jnp.tile(padded, (1, length))
    return tiled[:, : length * (2 * length - 1)].reshape(group_count, length, 2 * length - 1)


def gather_by_permutes(x, axis):
    count = lax.axis_size(axis)
    me = lax.axis_index(axis)
    pieces = [x]
    for by in range(1, count):
        pairs = [(s, (s + by) % count) for s in range(count)]
        pieces.append(lax.ppermute(x, axis, pairs))
    stacked = jnp.stack(pieces[::-1], axis=0)
    return jnp.roll(stacked, me + 1, axis=0)


def body(tokens, norm_gain, w_in, short_taps, rates, residues, w_out):
    tok_rows = tokens.shape[0]
    local_width = w_in.shape[2]
    local_groups = rates.shape[0]
    group_size = local_width // local_groups
    block_rows = BLOCK
    reach = block_rows - 1
    mode_count = rates.shape[1]
    highest = lax.Precision.HIGHEST
    n_ctx = lax.axis_size("ctx")
    n_grp = lax.axis_size("grp")
    me_ctx = lax.axis_index("ctx")
    me_grp = lax.axis_index("grp")
    shard_rows = w_in.shape[0]
    piece = shard_rows // n_grp
    streams = w_in.shape[1]

    span = short_taps.shape[0]
    halo = span - 1
    decay = rates[:, :, None]
    coef = residues * jnp.sqrt(-jnp.expm1(-2.0 * rates)) * mode_count ** (-0.5)
    lags = jnp.arange(block_rows).astype(jnp.float32)
    powers = jnp.exp(-decay * lags)
    long_taps = jnp.einsum("gn,gnt->gt", coef, powers, precision=highest)
    kernel = banded(long_taps[:, ::-1])[:, :, reach:]
    tail = jnp.exp(-decay * (reach - lags))
    entry = coef[:, None, :] * jnp.exp(-rates[:, None, :] * (lags[None, :, None] + 1.0))

    own = lax.dynamic_slice_in_dim(w_in, me_grp * piece, piece, axis=0)
    order = [0, 2, 1] if streams == 3 else list(range(streams))
    relayed = {}
    for s in order:
        got = lax.all_gather(own[:, s, :], "ctx", axis=0)
        if s == order[0]:
            got, kernel, tail, entry = lax.optimization_barrier((got, kernel, tail, entry))
        doubled = jnp.concatenate([got, got], axis=0)
        send = lax.dynamic_slice_in_dim(doubled, me_ctx + 1, n_ctx - 1, axis=0)
        received = []
        for by in range(1, n_grp):
            pairs = [(q, (q + by) % n_grp) for q in range(n_grp)]
            received.append(lax.ppermute(send, "grp", pairs))
        relayed[s] = (got, received)

    before = shifted(tokens[tok_rows - halo :], "ctx", 1)
    with_gain = jnp.concatenate([before, tokens, norm_gain[None]], axis=0)
    stacked = gather_by_permutes(with_gain, "tp")
    gathered = jnp.concatenate(list(stacked), axis=1)
    ext_rows = tok_rows + halo
    values = gathered[:ext_rows].astype(jnp.float32)
    gain_whole = gathered[ext_rows]
    scale = lax.rsqrt(jnp.mean(values * values, axis=1, keepdims=True) + 1e-06)
    normed = (values * scale * gain_whole.astype(jnp.float32)).astype(jnp.bfloat16)
    normed4 = normed.reshape(ext_rows, n_ctx, n_grp, piece)
    mine = lax.dynamic_index_in_dim(normed4, me_grp, axis=2, keepdims=False)
    others = []
    for by in range(1, n_grp):
        src_grp = (me_grp - by) % n_grp
        part = lax.dynamic_index_in_dim(normed4, src_grp, axis=2, keepdims=False)
        others.append((src_grp, jnp.roll(part, -me_ctx, axis=1)))
    filtered = {}
    for s in order:
        got, received = relayed[s]
        acc = jnp.einsum("tkr,krc->tc", mine, got, preferred_element_type=jnp.float32)
        for (src_grp, part), recv in zip(others, received):
            local = lax.dynamic_slice_in_dim(w_in[:, s, :], src_grp * piece, piece, axis=0)
            acc = acc + jnp.dot(part[:, 0], local, preferred_element_type=jnp.float32)
            acc = acc + jnp.einsum(
                "tkr,krc->tc", part[:, 1:], recv, preferred_element_type=jnp.float32
            )
        filtered[s] = short_filter(acc.astype(jnp.bfloat16), short_taps[:, s, :], tok_rows)
    product = filtered[0] * filtered[2]
    second = filtered[1]
    blocks = tok_rows // block_rows
    current = product.reshape(blocks, block_rows, local_groups, group_size)
    near = jnp.einsum("gij,bjgc->bigc", kernel, current, precision=highest)
    ends = jnp.einsum("gni,bigc->bgnc", tail, current, precision=highest)
    step_decay = jnp.exp(-decay * block_rows)

    def advance(state, end_block):
        return (step_decay * state + end_block, state)

    zero_state = jnp.zeros((local_groups, mode_count, group_size), jnp.float32)
    own_state, local_starts = lax.scan(advance, zero_state, ends)
    incoming = jnp.zeros_like(own_state)
    for by in range(1, n_ctx):
        pairs = [(k, k + by) for k in range(n_ctx - by)]
        arrived = lax.ppermute(own_state, "ctx", pairs)
        incoming = incoming + jnp.exp(-decay * (tok_rows * (by - 1.0))) * arrived
    block_index = jnp.arange(blocks).astype(jnp.float32)
    lead = jnp.exp(-decay[None] * block_rows * block_index[:, None, None, None])
    starts = lead * incoming[None] + local_starts
    distant = jnp.einsum("gin,bgnc->bigc", entry, starts, precision=highest)
    conv_out = (near + distant).reshape(tok_rows, local_width)
    gated = (second * conv_out).astype(jnp.bfloat16)
    mixed = jnp.dot(
        lax.all_gather(gated, "tp", axis=1, tiled=True), w_out, preferred_element_type=jnp.float32
    )
    return (tokens.astype(jnp.float32) + mixed).astype(jnp.bfloat16)


def solution(mesh):
    in_specs = (
        P(("grp", "ctx"), "tp"),
        P("tp"),
        P("ctx", None, "tp"),
        P(None, None, "tp"),
        P("tp", None),
        P("tp", None),
        P(None, "tp"),
    )
    out_specs = P(("grp", "ctx"), "tp")
    return jax.shard_map(body, mesh=mesh, in_specs=in_specs, out_specs=out_specs, check_vma=False)
```

```python
import jax
import jax.numpy as jnp
from jax import lax
from jax.sharding import PartitionSpec as P

BLOCK = 128


def shifted(x, axis, by):
    count = lax.axis_size(axis)
    pairs = [(i, i + by) for i in range(count) if 0 <= i + by < count]
    return lax.ppermute(x, axis, pairs)


def short_filter(extended, taps, count):
    values = extended.astype(jnp.float32)
    result = jnp.zeros((count, values.shape[1]), jnp.float32)
    span = taps.shape[0]
    for tap_index in range(span):
        begin = span - 1 - tap_index
        result = result + taps[tap_index] * values[begin : begin + count]
    return result


def banded(series):
    group_count, length = series.shape
    padded = jnp.concatenate([series, jnp.zeros_like(series)], axis=1)
    tiled = jnp.tile(padded, (1, length))
    return tiled[:, : length * (2 * length - 1)].reshape(group_count, length, 2 * length - 1)


def gather_by_permutes(x, axis):
    count = lax.axis_size(axis)
    me = lax.axis_index(axis)
    pieces = [x]
    for by in range(1, count):
        pairs = [(s, (s + by) % count) for s in range(count)]
        pieces.append(lax.ppermute(x, axis, pairs))
    stacked = jnp.stack(pieces[::-1], axis=0)
    return jnp.roll(stacked, me + 1, axis=0)


def body(tokens, norm_gain, w_in, short_taps, rates, residues, w_out):
    tok_rows = tokens.shape[0]
    local_width = w_in.shape[2]
    local_groups = rates.shape[0]
    group_size = local_width // local_groups
    block_rows = BLOCK
    reach = block_rows - 1
    mode_count = rates.shape[1]
    highest = lax.Precision.HIGHEST
    n_ctx = lax.axis_size("ctx")
    n_grp = lax.axis_size("grp")
    me_ctx = lax.axis_index("ctx")
    me_grp = lax.axis_index("grp")
    shard_rows = w_in.shape[0]
    piece = shard_rows // n_grp
    streams = w_in.shape[1]

    span = short_taps.shape[0]
    halo = span - 1
    decay = rates[:, :, None]
    coef = residues * jnp.sqrt(-jnp.expm1(-2.0 * rates)) * mode_count ** (-0.5)
    lags = jnp.arange(block_rows).astype(jnp.float32)
    powers = jnp.exp(-decay * lags)
    long_taps = jnp.einsum("gn,gnt->gt", coef, powers, precision=highest)
    kernel = banded(long_taps[:, ::-1])[:, :, reach:]
    tail = jnp.exp(-decay * (reach - lags))
    entry = coef[:, None, :] * jnp.exp(-rates[:, None, :] * (lags[None, :, None] + 1.0))

    own = lax.dynamic_slice_in_dim(w_in, me_grp * piece, piece, axis=0)
    order = [0, 2, 1] if streams == 3 else list(range(streams))
    relayed = {}
    for s in order:
        got = lax.all_gather(own[:, s, :], "ctx", axis=0)
        if s == order[0]:
            got, kernel, tail, entry = lax.optimization_barrier((got, kernel, tail, entry))
        doubled = jnp.concatenate([got, got], axis=0)
        send = lax.dynamic_slice_in_dim(doubled, me_ctx + 1, n_ctx - 1, axis=0)
        received = []
        for by in range(1, n_grp):
            pairs = [(q, (q + by) % n_grp) for q in range(n_grp)]
            received.append(lax.ppermute(send, "grp", pairs))
        relayed[s] = (got, received)

    before = shifted(tokens[tok_rows - halo :], "ctx", 1)
    with_gain = jnp.concatenate([before, tokens, norm_gain[None]], axis=0)
    stacked = gather_by_permutes(with_gain, "tp")
    gathered = jnp.concatenate(list(stacked), axis=1)
    ext_rows = tok_rows + halo
    values = gathered[:ext_rows].astype(jnp.float32)
    gain_whole = gathered[ext_rows]
    scale = lax.rsqrt(jnp.mean(values * values, axis=1, keepdims=True) + 1e-06)
    normed = (values * scale * gain_whole.astype(jnp.float32)).astype(jnp.bfloat16)
    normed4 = normed.reshape(ext_rows, n_ctx, n_grp, piece)
    mine = lax.dynamic_index_in_dim(normed4, me_grp, axis=2, keepdims=False)
    others = []
    for by in range(1, n_grp):
        src_grp = (me_grp - by) % n_grp
        part = lax.dynamic_index_in_dim(normed4, src_grp, axis=2, keepdims=False)
        others.append((src_grp, jnp.roll(part, -me_ctx, axis=1)))
    def project(s, received):
        got = relayed[s][0]
        acc = jnp.einsum("tkr,krc->tc", mine, got, preferred_element_type=jnp.float32)
        for (src_grp, part), recv in zip(others, received):
            local = lax.dynamic_slice_in_dim(w_in[:, s, :], src_grp * piece, piece, axis=0)
            acc = acc + jnp.dot(part[:, 0], local, preferred_element_type=jnp.float32)
            acc = acc + jnp.einsum(
                "tkr,krc->tc", part[:, 1:], recv, preferred_element_type=jnp.float32
            )
        rounded = lax.reduce_precision(acc, exponent_bits=8, mantissa_bits=7)
        return short_filter(rounded, short_taps[:, s, :], tok_rows)

    last = order[-1]
    filtered = {s: project(s, relayed[s][1]) for s in order[:-1]}
    product = filtered[0] * filtered[2]
    blocks = tok_rows // block_rows
    current = product.reshape(blocks, block_rows, local_groups, group_size)
    near = jnp.einsum("gij,bjgc->bigc", kernel, current, precision=highest)
    ends = jnp.einsum("gni,bigc->bgnc", tail, current, precision=highest)
    step_decay = jnp.exp(-decay * block_rows)

    def advance(state, end_block):
        return (step_decay * state + end_block, state)

    zero_state = jnp.zeros((local_groups, mode_count, group_size), jnp.float32)
    own_state, local_starts = lax.scan(advance, zero_state, ends)
    incoming = jnp.zeros_like(own_state)
    for by in range(1, n_ctx):
        pairs = [(k, k + by) for k in range(n_ctx - by)]
        arrived = lax.ppermute(own_state, "ctx", pairs)
        incoming = incoming + jnp.exp(-decay * (tok_rows * (by - 1.0))) * arrived
    block_index = jnp.arange(blocks).astype(jnp.float32)
    lead = jnp.exp(-decay[None] * block_rows * block_index[:, None, None, None])
    starts = lead * incoming[None] + local_starts
    distant = jnp.einsum("gin,bgnc->bigc", entry, starts, precision=highest)
    conv_out = (near + distant).reshape(tok_rows, local_width)
    late, conv_out = lax.optimization_barrier((relayed[last][1], conv_out))
    second = project(last, late)
    gated = (second * conv_out).astype(jnp.bfloat16)
    mixed = jnp.dot(
        lax.all_gather(gated, "tp", axis=1, tiled=True), w_out, preferred_element_type=jnp.float32
    )
    return (tokens.astype(jnp.float32) + mixed).astype(jnp.bfloat16)


def solution(mesh):
    in_specs = (
        P(("grp", "ctx"), "tp"),
        P("tp"),
        P("ctx", None, "tp"),
        P(None, None, "tp"),
        P("tp", None),
        P("tp", None),
        P(None, "tp"),
    )
    out_specs = P(("grp", "ctx"), "tp")
    return jax.shard_map(body, mesh=mesh, in_specs=in_specs, out_specs=out_specs, check_vma=False)
```

```python
import jax
import jax.numpy as jnp
from jax import lax
from jax.sharding import PartitionSpec as P

BLOCK = 128


def shifted(x, axis, by):
    count = lax.axis_size(axis)
    pairs = [(i, i + by) for i in range(count) if 0 <= i + by < count]
    return lax.ppermute(x, axis, pairs)


def short_filter(extended, taps, count):
    values = extended.astype(jnp.float32)
    result = jnp.zeros((count, values.shape[1]), jnp.float32)
    span = taps.shape[0]
    for tap_index in range(span):
        begin = span - 1 - tap_index
        result = result + taps[tap_index] * values[begin : begin + count]
    return result


def banded(series):
    group_count, length = series.shape
    padded = jnp.concatenate([series, jnp.zeros_like(series)], axis=1)
    tiled = jnp.tile(padded, (1, length))
    return tiled[:, : length * (2 * length - 1)].reshape(group_count, length, 2 * length - 1)


def gather_by_permutes(x, axis):
    count = lax.axis_size(axis)
    me = lax.axis_index(axis)
    pieces = [x]
    for by in range(1, count):
        pairs = [(s, (s + by) % count) for s in range(count)]
        pieces.append(lax.ppermute(x, axis, pairs))
    stacked = jnp.stack(pieces[::-1], axis=0)
    return jnp.roll(stacked, me + 1, axis=0)


def gather_by_swaps(x, axis):
    count = lax.axis_size(axis)
    me = lax.axis_index(axis)
    bits = []
    b = 1
    while b < count:
        bits.append(b)
        b *= 2
    if 2 ** len(bits) != count:
        return lax.all_gather(x, axis, axis=0)
    held = x[None]
    masks = [0]
    for bit in bits[::-1]:
        pairs = [(q, q ^ bit) for q in range(count)]
        held = jnp.concatenate([held, lax.ppermute(held, axis, pairs)], axis=0)
        masks = masks + [m ^ bit for m in masks]
    inverse = [masks.index(m) for m in range(count)]
    table = jnp.array(inverse, jnp.int32)
    where = jnp.take(table, jnp.bitwise_xor(jnp.arange(count, dtype=jnp.int32), me))
    return jnp.take(held, where, axis=0)


def body(tokens, norm_gain, w_in, short_taps, rates, residues, w_out):
    tok_rows = tokens.shape[0]
    local_width = w_in.shape[2]
    local_groups = rates.shape[0]
    group_size = local_width // local_groups
    block_rows = BLOCK
    reach = block_rows - 1
    mode_count = rates.shape[1]
    highest = lax.Precision.HIGHEST
    n_ctx = lax.axis_size("ctx")
    n_grp = lax.axis_size("grp")
    me_ctx = lax.axis_index("ctx")
    me_grp = lax.axis_index("grp")
    shard_rows = w_in.shape[0]
    piece = shard_rows // n_grp
    streams = w_in.shape[1]

    span = short_taps.shape[0]
    halo = span - 1
    decay = rates[:, :, None]
    coef = residues * jnp.sqrt(-jnp.expm1(-2.0 * rates)) * mode_count ** (-0.5)
    lags = jnp.arange(block_rows).astype(jnp.float32)
    powers = jnp.exp(-decay * lags)
    long_taps = jnp.einsum("gn,gnt->gt", coef, powers, precision=highest)
    kernel = banded(long_taps[:, ::-1])[:, :, reach:]
    tail = jnp.exp(-decay * (reach - lags))
    entry = coef[:, None, :] * jnp.exp(-rates[:, None, :] * (lags[None, :, None] + 1.0))

    own = lax.dynamic_slice_in_dim(w_in, me_grp * piece, piece, axis=0)
    order = [0, 2, 1] if streams == 3 else list(range(streams))
    relayed = {}
    for s in order:
        got = lax.all_gather(own[:, s, :], "ctx", axis=0)
        if s == order[0]:
            got, kernel, tail, entry = lax.optimization_barrier((got, kernel, tail, entry))
        doubled = jnp.concatenate([got, got], axis=0)
        send = lax.dynamic_slice_in_dim(doubled, me_ctx + 1, n_ctx - 1, axis=0)
        received = []
        for by in range(1, n_grp):
            pairs = [(q, (q + by) % n_grp) for q in range(n_grp)]
            received.append(lax.ppermute(send, "grp", pairs))
        relayed[s] = (got, received)

    before = shifted(tokens[tok_rows - halo :], "ctx", 1)
    with_gain = jnp.concatenate([before, tokens, norm_gain[None]], axis=0)
    stacked = gather_by_permutes(with_gain, "tp")
    gathered = jnp.concatenate(list(stacked), axis=1)
    ext_rows = tok_rows + halo
    values = gathered[:ext_rows].astype(jnp.float32)
    gain_whole = gathered[ext_rows]
    scale = lax.rsqrt(jnp.mean(values * values, axis=1, keepdims=True) + 1e-06)
    normed = (values * scale * gain_whole.astype(jnp.float32)).astype(jnp.bfloat16)
    normed4 = normed.reshape(ext_rows, n_ctx, n_grp, piece)
    mine = lax.dynamic_index_in_dim(normed4, me_grp, axis=2, keepdims=False)
    others = []
    for by in range(1, n_grp):
        src_grp = (me_grp - by) % n_grp
        part = lax.dynamic_index_in_dim(normed4, src_grp, axis=2, keepdims=False)
        others.append((src_grp, jnp.roll(part, -me_ctx, axis=1)))
    def project(s, received):
        got = relayed[s][0]
        acc = jnp.einsum("tkr,krc->tc", mine, got, preferred_element_type=jnp.float32)
        for (src_grp, part), recv in zip(others, received):
            local = lax.dynamic_slice_in_dim(w_in[:, s, :], src_grp * piece, piece, axis=0)
            acc = acc + jnp.dot(part[:, 0], local, preferred_element_type=jnp.float32)
            acc = acc + jnp.einsum(
                "tkr,krc->tc", part[:, 1:], recv, preferred_element_type=jnp.float32
            )
        rounded = lax.reduce_precision(acc, exponent_bits=8, mantissa_bits=7)
        return short_filter(rounded, short_taps[:, s, :], tok_rows)

    last = order[-1]
    filtered = {s: project(s, relayed[s][1]) for s in order[:-1]}
    product = filtered[0] * filtered[2]
    blocks = tok_rows // block_rows
    current = product.reshape(blocks, block_rows, local_groups, group_size)
    near = jnp.einsum("gij,bjgc->bigc", kernel, current, precision=highest)
    ends = jnp.einsum("gni,bigc->bgnc", tail, current, precision=highest)
    step_decay = jnp.exp(-decay * block_rows)

    def advance(state, end_block):
        return (step_decay * state + end_block, state)

    zero_state = jnp.zeros((local_groups, mode_count, group_size), jnp.float32)
    own_state, local_starts = lax.scan(advance, zero_state, ends)
    incoming = jnp.zeros_like(own_state)
    for by in range(1, n_ctx):
        pairs = [(k, k + by) for k in range(n_ctx - by)]
        arrived = lax.ppermute(own_state, "ctx", pairs)
        incoming = incoming + jnp.exp(-decay * (tok_rows * (by - 1.0))) * arrived
    block_index = jnp.arange(blocks).astype(jnp.float32)
    lead = jnp.exp(-decay[None] * block_rows * block_index[:, None, None, None])
    starts = lead * incoming[None] + local_starts
    distant = jnp.einsum("gin,bgnc->bigc", entry, starts, precision=highest)
    conv_out = (near + distant).reshape(tok_rows, local_width)
    late, conv_out = lax.optimization_barrier((relayed[last][1], conv_out))
    second = project(last, late)
    gated = (second * conv_out).astype(jnp.bfloat16)
    pieces = gather_by_swaps(gated, "tp")
    mixed = jnp.einsum("qtc,qcf->tf", pieces, w_out.reshape(pieces.shape[0], local_width, -1),
                       preferred_element_type=jnp.float32)
    return (tokens.astype(jnp.float32) + mixed).astype(jnp.bfloat16)


def solution(mesh):
    in_specs = (
        P(("grp", "ctx"), "tp"),
        P("tp"),
        P("ctx", None, "tp"),
        P(None, None, "tp"),
        P("tp", None),
        P("tp", None),
        P(None, "tp"),
    )
    out_specs = P(("grp", "ctx"), "tp")
    return jax.shard_map(body, mesh=mesh, in_specs=in_specs, out_specs=out_specs, check_vma=False)
```

```python
import jax
import jax.numpy as jnp
from jax import lax
from jax.sharding import PartitionSpec as P

BLOCK = 128


def shifted(x, axis, by):
    count = lax.axis_size(axis)
    pairs = [(i, i + by) for i in range(count) if 0 <= i + by < count]
    return lax.ppermute(x, axis, pairs)


def short_filter(extended, taps, count):
    values = extended.astype(jnp.float32)
    result = jnp.zeros((count, values.shape[1]), jnp.float32)
    span = taps.shape[0]
    for tap_index in range(span):
        begin = span - 1 - tap_index
        result = result + taps[tap_index] * values[begin : begin + count]
    return result


def banded(series):
    group_count, length = series.shape
    padded = jnp.concatenate([series, jnp.zeros_like(series)], axis=1)
    tiled = jnp.tile(padded, (1, length))
    return tiled[:, : length * (2 * length - 1)].reshape(group_count, length, 2 * length - 1)


def gather_by_permutes(x, axis):
    count = lax.axis_size(axis)
    me = lax.axis_index(axis)
    pieces = [x]
    for by in range(1, count):
        pairs = [(s, (s + by) % count) for s in range(count)]
        pieces.append(lax.ppermute(x, axis, pairs))
    stacked = jnp.stack(pieces[::-1], axis=0)
    return jnp.roll(stacked, me + 1, axis=0)


def gather_by_swaps(x, axis):
    count = lax.axis_size(axis)
    me = lax.axis_index(axis)
    bits = []
    b = 1
    while b < count:
        bits.append(b)
        b *= 2
    if 2 ** len(bits) != count:
        return lax.all_gather(x, axis, axis=0)
    held = x[None]
    masks = [0]
    for bit in bits[::-1]:
        pairs = [(q, q ^ bit) for q in range(count)]
        held = jnp.concatenate([held, lax.ppermute(held, axis, pairs)], axis=0)
        masks = masks + [m ^ bit for m in masks]
    inverse = [masks.index(m) for m in range(count)]
    table = jnp.array(inverse, jnp.int32)
    where = jnp.take(table, jnp.bitwise_xor(jnp.arange(count, dtype=jnp.int32), me))
    return jnp.take(held, where, axis=0)


def body(tokens, norm_gain, w_in, short_taps, rates, residues, w_out):
    tok_rows = tokens.shape[0]
    local_width = w_in.shape[2]
    local_groups = rates.shape[0]
    group_size = local_width // local_groups
    block_rows = BLOCK
    reach = block_rows - 1
    mode_count = rates.shape[1]
    highest = lax.Precision.HIGHEST
    n_ctx = lax.axis_size("ctx")
    n_grp = lax.axis_size("grp")
    me_ctx = lax.axis_index("ctx")
    me_grp = lax.axis_index("grp")
    shard_rows = w_in.shape[0]
    piece = shard_rows // n_grp
    streams = w_in.shape[1]

    span = short_taps.shape[0]
    halo = span - 1
    decay = rates[:, :, None]
    coef = residues * jnp.sqrt(-jnp.expm1(-2.0 * rates)) * mode_count ** (-0.5)
    lags = jnp.arange(block_rows).astype(jnp.float32)
    powers = jnp.exp(-decay * lags)
    long_taps = jnp.einsum("gn,gnt->gt", coef, powers, precision=highest)
    kernel = banded(long_taps[:, ::-1])[:, :, reach:]
    tail = jnp.exp(-decay * (reach - lags))
    entry = coef[:, None, :] * jnp.exp(-rates[:, None, :] * (lags[None, :, None] + 1.0))

    own = lax.dynamic_slice_in_dim(w_in, me_grp * piece, piece, axis=0)
    if streams == 3 and local_width % 256 == 0:
        half = local_width // 2
        order = [(0, 0, local_width), (2, 0, local_width), (1, 0, half), (1, half, half)]
    else:
        order = [(s, 0, local_width) for s in range(streams)]
    relayed = {}
    previous = None
    for index, chunk in enumerate(order):
        s, c0, cn = chunk
        operand = own[:, s, c0 : c0 + cn]
        if index >= 2:
            operand, _ = lax.optimization_barrier((operand, previous))
        got = lax.all_gather(operand, "ctx", axis=0)
        previous = got
        if chunk == order[0]:
            got, kernel, tail, entry = lax.optimization_barrier((got, kernel, tail, entry))
        doubled = jnp.concatenate([got, got], axis=0)
        send = lax.dynamic_slice_in_dim(doubled, me_ctx + 1, n_ctx - 1, axis=0)
        received = []
        for by in range(1, n_grp):
            pairs = [(q, (q + by) % n_grp) for q in range(n_grp)]
            received.append(lax.ppermute(send, "grp", pairs))
        relayed[chunk] = (got, received)

    before = shifted(tokens[tok_rows - halo :], "ctx", 1)
    with_gain = jnp.concatenate([before, tokens, norm_gain[None]], axis=0)
    stacked = gather_by_permutes(with_gain, "tp")
    gathered = jnp.concatenate(list(stacked), axis=1)
    ext_rows = tok_rows + halo
    values = gathered[:ext_rows].astype(jnp.float32)
    gain_whole = gathered[ext_rows]
    scale = lax.rsqrt(jnp.mean(values * values, axis=1, keepdims=True) + 1e-06)
    normed = (values * scale * gain_whole.astype(jnp.float32)).astype(jnp.bfloat16)
    normed4 = normed.reshape(ext_rows, n_ctx, n_grp, piece)
    mine = lax.dynamic_index_in_dim(normed4, me_grp, axis=2, keepdims=False)
    others = []
    for by in range(1, n_grp):
        src_grp = (me_grp - by) % n_grp
        part = lax.dynamic_index_in_dim(normed4, src_grp, axis=2, keepdims=False)
        others.append((src_grp, jnp.roll(part, -me_ctx, axis=1)))
    def project(chunk, received):
        s, c0, cn = chunk
        got = relayed[chunk][0]
        acc = jnp.einsum("tkr,krc->tc", mine, got, preferred_element_type=jnp.float32)
        for (src_grp, part), recv in zip(others, received):
            local = lax.dynamic_slice_in_dim(w_in[:, s, c0 : c0 + cn], src_grp * piece, piece, axis=0)
            acc = acc + jnp.dot(part[:, 0], local, preferred_element_type=jnp.float32)
            acc = acc + jnp.einsum(
                "tkr,krc->tc", part[:, 1:], recv, preferred_element_type=jnp.float32
            )
        rounded = lax.reduce_precision(acc, exponent_bits=8, mantissa_bits=7)
        return short_filter(rounded, short_taps[:, s, c0 : c0 + cn], tok_rows)

    last = order[-1]
    filtered = {chunk: project(chunk, relayed[chunk][1]) for chunk in order[:-1]}

    def stream(s):
        return jnp.concatenate([filtered[c] for c in order if c[0] == s], axis=1)

    product = stream(0) * stream(2)
    blocks = tok_rows // block_rows
    current = product.reshape(blocks, block_rows, local_groups, group_size)
    near = jnp.einsum("gij,bjgc->bigc", kernel, current, precision=highest)
    ends = jnp.einsum("gni,bigc->bgnc", tail, current, precision=highest)
    step_decay = jnp.exp(-decay * block_rows)

    def advance(state, end_block):
        return (step_decay * state + end_block, state)

    zero_state = jnp.zeros((local_groups, mode_count, group_size), jnp.float32)
    own_state, local_starts = lax.scan(advance, zero_state, ends)
    incoming = jnp.zeros_like(own_state)
    for by in range(1, n_ctx):
        pairs = [(k, k + by) for k in range(n_ctx - by)]
        arrived = lax.ppermute(own_state, "ctx", pairs)
        incoming = incoming + jnp.exp(-decay * (tok_rows * (by - 1.0))) * arrived
    block_index = jnp.arange(blocks).astype(jnp.float32)
    lead = jnp.exp(-decay[None] * block_rows * block_index[:, None, None, None])
    starts = lead * incoming[None] + local_starts
    distant = jnp.einsum("gin,bgnc->bigc", entry, starts, precision=highest)
    conv_out = (near + distant).reshape(tok_rows, local_width)
    late, conv_out = lax.optimization_barrier((relayed[last][1], conv_out))
    filtered[last] = project(last, late)
    second = stream(1)
    gated = (second * conv_out).astype(jnp.bfloat16)
    pieces = gather_by_swaps(gated, "tp")
    mixed = jnp.einsum("qtc,qcf->tf", pieces, w_out.reshape(pieces.shape[0], local_width, -1),
                       preferred_element_type=jnp.float32)
    return (tokens.astype(jnp.float32) + mixed).astype(jnp.bfloat16)


def solution(mesh):
    in_specs = (
        P(("grp", "ctx"), "tp"),
        P("tp"),
        P("ctx", None, "tp"),
        P(None, None, "tp"),
        P("tp", None),
        P("tp", None),
        P(None, "tp"),
    )
    out_specs = P(("grp", "ctx"), "tp")
    return jax.shard_map(body, mesh=mesh, in_specs=in_specs, out_specs=out_specs, check_vma=False)
```

```python
import jax
import jax.numpy as jnp
from jax import lax
from jax.sharding import PartitionSpec as P

BLOCK = 128


def shifted(x, axis, by):
    count = lax.axis_size(axis)
    pairs = [(i, i + by) for i in range(count) if 0 <= i + by < count]
    return lax.ppermute(x, axis, pairs)


def short_filter(extended, taps, count):
    values = extended.astype(jnp.float32)
    result = jnp.zeros((count, values.shape[1]), jnp.float32)
    span = taps.shape[0]
    for tap_index in range(span):
        begin = span - 1 - tap_index
        result = result + taps[tap_index] * values[begin : begin + count]
    return result


def banded(series):
    group_count, length = series.shape
    padded = jnp.concatenate([series, jnp.zeros_like(series)], axis=1)
    tiled = jnp.tile(padded, (1, length))
    return tiled[:, : length * (2 * length - 1)].reshape(group_count, length, 2 * length - 1)


def gather_by_permutes(x, axis):
    count = lax.axis_size(axis)
    me = lax.axis_index(axis)
    pieces = [x]
    for by in range(1, count):
        pairs = [(s, (s + by) % count) for s in range(count)]
        pieces.append(lax.ppermute(x, axis, pairs))
    stacked = jnp.stack(pieces[::-1], axis=0)
    return jnp.roll(stacked, me + 1, axis=0)


def gather_by_swaps(x, axis):
    count = lax.axis_size(axis)
    me = lax.axis_index(axis)
    bits = []
    b = 1
    while b < count:
        bits.append(b)
        b *= 2
    if 2 ** len(bits) != count:
        return lax.all_gather(x, axis, axis=0)
    held = x[None]
    masks = [0]
    for bit in bits[::-1]:
        pairs = [(q, q ^ bit) for q in range(count)]
        held = jnp.concatenate([held, lax.ppermute(held, axis, pairs)], axis=0)
        masks = masks + [m ^ bit for m in masks]
    inverse = [masks.index(m) for m in range(count)]
    table = jnp.array(inverse, jnp.int32)
    where = jnp.take(table, jnp.bitwise_xor(jnp.arange(count, dtype=jnp.int32), me))
    return jnp.take(held, where, axis=0)


def body(tokens, norm_gain, w_in, short_taps, rates, residues, w_out):
    tok_rows = tokens.shape[0]
    local_width = w_in.shape[2]
    local_groups = rates.shape[0]
    group_size = local_width // local_groups
    block_rows = BLOCK
    reach = block_rows - 1
    mode_count = rates.shape[1]
    highest = lax.Precision.HIGHEST
    n_ctx = lax.axis_size("ctx")
    n_grp = lax.axis_size("grp")
    me_ctx = lax.axis_index("ctx")
    me_grp = lax.axis_index("grp")
    shard_rows = w_in.shape[0]
    piece = shard_rows // n_grp
    streams = w_in.shape[1]

    span = short_taps.shape[0]
    halo = span - 1
    decay = rates[:, :, None]
    coef = residues * jnp.sqrt(-jnp.expm1(-2.0 * rates)) * mode_count ** (-0.5)
    lags = jnp.arange(block_rows).astype(jnp.float32)
    powers = jnp.exp(-decay * lags)
    long_taps = jnp.einsum("gn,gnt->gt", coef, powers, precision=highest)
    kernel = banded(long_taps[:, ::-1])[:, :, reach:]
    tail = jnp.exp(-decay * (reach - lags))
    entry = coef[:, None, :] * jnp.exp(-rates[:, None, :] * (lags[None, :, None] + 1.0))

    with_gain = jnp.concatenate([tokens, norm_gain[None]], axis=0)
    stacked = gather_by_swaps(with_gain, "tp")
    whole_rows = jnp.concatenate(list(stacked), axis=1)
    before = shifted(whole_rows[tok_rows - halo : tok_rows], "ctx", 1)
    gathered = jnp.concatenate([before, whole_rows], axis=0)
    own = lax.dynamic_slice_in_dim(w_in, me_grp * piece, piece, axis=0)

    def relay_send(got):
        doubled = jnp.concatenate([got, got], axis=0)
        return lax.dynamic_slice_in_dim(doubled, me_ctx + 1, n_ctx - 1, axis=0)

    def relay(send):
        received = []
        for by in range(1, n_grp):
            pairs = [(q, (q + by) % n_grp) for q in range(n_grp)]
            received.append(lax.ppermute(send, "grp", pairs))
        return received

    order = [0, 2, 1] if streams == 3 else list(range(streams))
    relayed = {}
    for s in order:
        got = lax.all_gather(own[:, s, :], "ctx", axis=0)
        if s == order[0]:
            got, kernel, tail, entry = lax.optimization_barrier((got, kernel, tail, entry))
        if s == order[-1] and len(order) > 1:
            relayed[s] = (got, None)
            continue
        send = relay_send(got)
        if s == order[0]:
            send, gathered = lax.optimization_barrier((send, gathered))
        relayed[s] = (got, relay(send))

    ext_rows = tok_rows + halo
    values = gathered[:ext_rows].astype(jnp.float32)
    gain_whole = gathered[ext_rows]
    scale = lax.rsqrt(jnp.mean(values * values, axis=1, keepdims=True) + 1e-06)
    normed = (values * scale * gain_whole.astype(jnp.float32)).astype(jnp.bfloat16)
    normed4 = normed.reshape(ext_rows, n_ctx, n_grp, piece)
    mine = lax.dynamic_index_in_dim(normed4, me_grp, axis=2, keepdims=False)
    others = []
    for by in range(1, n_grp):
        src_grp = (me_grp - by) % n_grp
        part = lax.dynamic_index_in_dim(normed4, src_grp, axis=2, keepdims=False)
        others.append((src_grp, jnp.roll(part, -me_ctx, axis=1)))
    def project(s, received):
        got = relayed[s][0]
        acc = jnp.einsum("tkr,krc->tc", mine, got, preferred_element_type=jnp.float32)
        for (src_grp, part), recv in zip(others, received):
            local = lax.dynamic_slice_in_dim(w_in[:, s, :], src_grp * piece, piece, axis=0)
            acc = acc + jnp.dot(part[:, 0], local, preferred_element_type=jnp.float32)
            acc = acc + jnp.einsum(
                "tkr,krc->tc", part[:, 1:], recv, preferred_element_type=jnp.float32
            )
        rounded = lax.reduce_precision(acc, exponent_bits=8, mantissa_bits=7)
        return short_filter(rounded, short_taps[:, s, :], tok_rows)

    last = order[-1]
    filtered = {s: project(s, relayed[s][1]) for s in order[:-1]}
    first = order[0]
    if relayed[last][1] is None:
        filtered[first], tied = lax.optimization_barrier((filtered[first], relayed[last][0]))
        relayed[last] = (tied, relay(relay_send(tied)))
    product = filtered[0] * filtered[2]
    blocks = tok_rows // block_rows
    current = product.reshape(blocks, block_rows, local_groups, group_size)
    near = jnp.einsum("gij,bjgc->bigc", kernel, current, precision=highest)
    ends = jnp.einsum("gni,bigc->bgnc", tail, current, precision=highest)
    step_decay = jnp.exp(-decay * block_rows)

    def advance(state, end_block):
        return (step_decay * state + end_block, state)

    zero_state = jnp.zeros((local_groups, mode_count, group_size), jnp.float32)
    own_state, local_starts = lax.scan(advance, zero_state, ends)
    incoming = jnp.zeros_like(own_state)
    for by in range(1, n_ctx):
        pairs = [(k, k + by) for k in range(n_ctx - by)]
        arrived = lax.ppermute(own_state, "ctx", pairs)
        incoming = incoming + jnp.exp(-decay * (tok_rows * (by - 1.0))) * arrived
    block_index = jnp.arange(blocks).astype(jnp.float32)
    lead = jnp.exp(-decay[None] * block_rows * block_index[:, None, None, None])
    starts = lead * incoming[None] + local_starts
    distant = jnp.einsum("gin,bgnc->bigc", entry, starts, precision=highest)
    conv_out = (near + distant).reshape(tok_rows, local_width)
    late, conv_out = lax.optimization_barrier((relayed[last][1], conv_out))
    second = project(last, late)
    gated = (second * conv_out).astype(jnp.bfloat16)
    pieces = gather_by_swaps(gated, "tp")
    mixed = jnp.einsum("qtc,qcf->tf", pieces, w_out.reshape(pieces.shape[0], local_width, -1),
                       preferred_element_type=jnp.float32)
    return (tokens.astype(jnp.float32) + mixed).astype(jnp.bfloat16)


def solution(mesh):
    in_specs = (
        P(("grp", "ctx"), "tp"),
        P("tp"),
        P("ctx", None, "tp"),
        P(None, None, "tp"),
        P("tp", None),
        P("tp", None),
        P(None, "tp"),
    )
    out_specs = P(("grp", "ctx"), "tp")
    return jax.shard_map(body, mesh=mesh, in_specs=in_specs, out_specs=out_specs, check_vma=False)
```

```python
import jax
import jax.numpy as jnp
from jax import lax
from jax.sharding import PartitionSpec as P

BLOCK = 128


def shifted(x, axis, by):
    count = lax.axis_size(axis)
    pairs = [(i, i + by) for i in range(count) if 0 <= i + by < count]
    return lax.ppermute(x, axis, pairs)


def short_filter(extended, taps, count):
    values = extended.astype(jnp.float32)
    result = jnp.zeros((count, values.shape[1]), jnp.float32)
    span = taps.shape[0]
    for tap_index in range(span):
        begin = span - 1 - tap_index
        result = result + taps[tap_index] * values[begin : begin + count]
    return result


def banded(series):
    group_count, length = series.shape
    padded = jnp.concatenate([series, jnp.zeros_like(series)], axis=1)
    tiled = jnp.tile(padded, (1, length))
    return tiled[:, : length * (2 * length - 1)].reshape(group_count, length, 2 * length - 1)


def gather_by_permutes(x, axis):
    count = lax.axis_size(axis)
    me = lax.axis_index(axis)
    pieces = [x]
    for by in range(1, count):
        pairs = [(s, (s + by) % count) for s in range(count)]
        pieces.append(lax.ppermute(x, axis, pairs))
    stacked = jnp.stack(pieces[::-1], axis=0)
    return jnp.roll(stacked, me + 1, axis=0)


def gather_by_swaps(x, axis):
    count = lax.axis_size(axis)
    me = lax.axis_index(axis)
    bits = []
    b = 1
    while b < count:
        bits.append(b)
        b *= 2
    if 2 ** len(bits) != count:
        return lax.all_gather(x, axis, axis=0)
    held = x[None]
    masks = [0]
    for bit in bits[::-1]:
        pairs = [(q, q ^ bit) for q in range(count)]
        held = jnp.concatenate([held, lax.ppermute(held, axis, pairs)], axis=0)
        masks = masks + [m ^ bit for m in masks]
    inverse = [masks.index(m) for m in range(count)]
    table = jnp.array(inverse, jnp.int32)
    where = jnp.take(table, jnp.bitwise_xor(jnp.arange(count, dtype=jnp.int32), me))
    return jnp.take(held, where, axis=0)


def body(tokens, norm_gain, w_in, short_taps, rates, residues, w_out):
    tok_rows = tokens.shape[0]
    local_width = w_in.shape[2]
    local_groups = rates.shape[0]
    group_size = local_width // local_groups
    block_rows = BLOCK
    reach = block_rows - 1
    mode_count = rates.shape[1]
    highest = lax.Precision.HIGHEST
    n_ctx = lax.axis_size("ctx")
    n_grp = lax.axis_size("grp")
    me_ctx = lax.axis_index("ctx")
    me_grp = lax.axis_index("grp")
    shard_rows = w_in.shape[0]
    piece = shard_rows // n_grp
    streams = w_in.shape[1]

    span = short_taps.shape[0]
    halo = span - 1
    decay = rates[:, :, None]
    coef = residues * jnp.sqrt(-jnp.expm1(-2.0 * rates)) * mode_count ** (-0.5)
    lags = jnp.arange(block_rows).astype(jnp.float32)
    powers = jnp.exp(-decay * lags)
    long_taps = jnp.einsum("gn,gnt->gt", coef, powers, precision=highest)
    kernel = banded(long_taps[:, ::-1])[:, :, reach:]
    tail = jnp.exp(-decay * (reach - lags))
    entry = coef[:, None, :] * jnp.exp(-rates[:, None, :] * (lags[None, :, None] + 1.0))

    with_gain = jnp.concatenate([tokens, norm_gain[None]], axis=0)
    stacked = gather_by_swaps(with_gain, "tp")
    whole_rows = jnp.concatenate(list(stacked), axis=1)
    before = shifted(whole_rows[tok_rows - halo : tok_rows], "ctx", 1)
    gathered = jnp.concatenate([before, whole_rows], axis=0)
    own = lax.dynamic_slice_in_dim(w_in, me_grp * piece, piece, axis=0)

    def relay_send(got):
        doubled = jnp.concatenate([got, got], axis=0)
        return lax.dynamic_slice_in_dim(doubled, me_ctx + 1, n_ctx - 1, axis=0)

    def relay(send):
        received = []
        for by in range(1, n_grp):
            pairs = [(q, (q + by) % n_grp) for q in range(n_grp)]
            received.append(lax.ppermute(send, "grp", pairs))
        return received

    order = [0, 2, 1] if streams == 3 else list(range(streams))
    relayed = {}
    for s in order:
        got = lax.all_gather(own[:, s, :], "ctx", axis=0)
        if s == order[0]:
            got, kernel, tail, entry = lax.optimization_barrier((got, kernel, tail, entry))
        if s == order[-1] and len(order) > 1:
            relayed[s] = (got, None)
            continue
        send = relay_send(got)
        if s == order[0]:
            send, gathered = lax.optimization_barrier((send, gathered))
        relayed[s] = (got, relay(send))

    ext_rows = tok_rows + halo
    values = gathered[:ext_rows].astype(jnp.float32)
    gain_whole = gathered[ext_rows]
    scale = lax.rsqrt(jnp.mean(values * values, axis=1, keepdims=True) + 1e-06)
    normed = (values * scale * gain_whole.astype(jnp.float32)).astype(jnp.bfloat16)
    blocks = normed.reshape(ext_rows, n_ctx * n_grp, piece).transpose(1, 0, 2)
    shard_ids = jnp.arange(n_ctx, dtype=jnp.int32)
    mine = jnp.take(blocks, shard_ids * n_grp + me_grp, axis=0)
    others = []
    for by in range(1, n_grp):
        src_grp = (me_grp - by) % n_grp
        rolled = ((shard_ids + me_ctx) % n_ctx) * n_grp + src_grp
        others.append((src_grp, jnp.take(blocks, rolled, axis=0)))
    def project(s, received):
        got = relayed[s][0]
        acc = jnp.einsum("ktr,krc->tc", mine, got, preferred_element_type=jnp.float32)
        for (src_grp, part), recv in zip(others, received):
            local = lax.dynamic_slice_in_dim(w_in[:, s, :], src_grp * piece, piece, axis=0)
            acc = acc + jnp.dot(part[0], local, preferred_element_type=jnp.float32)
            acc = acc + jnp.einsum(
                "ktr,krc->tc", part[1:], recv, preferred_element_type=jnp.float32
            )
        rounded = lax.reduce_precision(acc, exponent_bits=8, mantissa_bits=7)
        return short_filter(rounded, short_taps[:, s, :], tok_rows)

    last = order[-1]
    filtered = {s: project(s, relayed[s][1]) for s in order[:-1]}
    first = order[0]
    if relayed[last][1] is None:
        filtered[first], tied = lax.optimization_barrier((filtered[first], relayed[last][0]))
        relayed[last] = (tied, relay(relay_send(tied)))
    product = filtered[0] * filtered[2]
    blocks = tok_rows // block_rows
    current = product.reshape(blocks, block_rows, local_groups, group_size)
    near = jnp.einsum("gij,bjgc->bigc", kernel, current, precision=highest)
    ends = jnp.einsum("gni,bigc->bgnc", tail, current, precision=highest)
    step_decay = jnp.exp(-decay * block_rows)

    def advance(state, end_block):
        return (step_decay * state + end_block, state)

    zero_state = jnp.zeros((local_groups, mode_count, group_size), jnp.float32)
    own_state, local_starts = lax.scan(advance, zero_state, ends)
    incoming = jnp.zeros_like(own_state)
    for by in range(1, n_ctx):
        pairs = [(k, k + by) for k in range(n_ctx - by)]
        arrived = lax.ppermute(own_state, "ctx", pairs)
        incoming = incoming + jnp.exp(-decay * (tok_rows * (by - 1.0))) * arrived
    block_index = jnp.arange(blocks).astype(jnp.float32)
    lead = jnp.exp(-decay[None] * block_rows * block_index[:, None, None, None])
    starts = lead * incoming[None] + local_starts
    distant = jnp.einsum("gin,bgnc->bigc", entry, starts, precision=highest)
    conv_out = (near + distant).reshape(tok_rows, local_width)
    late, conv_out = lax.optimization_barrier((relayed[last][1], conv_out))
    second = project(last, late)
    gated = (second * conv_out).astype(jnp.bfloat16)
    pieces = gather_by_swaps(gated, "tp")
    mixed = jnp.einsum("qtc,qcf->tf", pieces, w_out.reshape(pieces.shape[0], local_width, -1),
                       preferred_element_type=jnp.float32)
    return (tokens.astype(jnp.float32) + mixed).astype(jnp.bfloat16)


def solution(mesh):
    in_specs = (
        P(("grp", "ctx"), "tp"),
        P("tp"),
        P("ctx", None, "tp"),
        P(None, None, "tp"),
        P("tp", None),
        P("tp", None),
        P(None, "tp"),
    )
    out_specs = P(("grp", "ctx"), "tp")
    return jax.shard_map(body, mesh=mesh, in_specs=in_specs, out_specs=out_specs, check_vma=False)
```

```python
import jax
import jax.numpy as jnp
from jax import lax
from jax.sharding import PartitionSpec as P

BLOCK = 128


def shifted(x, axis, by):
    count = lax.axis_size(axis)
    pairs = [(i, i + by) for i in range(count) if 0 <= i + by < count]
    return lax.ppermute(x, axis, pairs)


def short_filter(extended, taps, count):
    values = extended.astype(jnp.float32)
    result = jnp.zeros((count, values.shape[1]), jnp.float32)
    span = taps.shape[0]
    for tap_index in range(span):
        begin = span - 1 - tap_index
        result = result + taps[tap_index] * values[begin : begin + count]
    return result


def banded(series):
    group_count, length = series.shape
    padded = jnp.concatenate([series, jnp.zeros_like(series)], axis=1)
    tiled = jnp.tile(padded, (1, length))
    return tiled[:, : length * (2 * length - 1)].reshape(group_count, length, 2 * length - 1)


def gather_by_permutes(x, axis):
    count = lax.axis_size(axis)
    me = lax.axis_index(axis)
    pieces = [x]
    for by in range(1, count):
        pairs = [(s, (s + by) % count) for s in range(count)]
        pieces.append(lax.ppermute(x, axis, pairs))
    stacked = jnp.stack(pieces[::-1], axis=0)
    return jnp.roll(stacked, me + 1, axis=0)


def gather_by_swaps(x, axis):
    count = lax.axis_size(axis)
    me = lax.axis_index(axis)
    bits = []
    b = 1
    while b < count:
        bits.append(b)
        b *= 2
    if 2 ** len(bits) != count:
        return lax.all_gather(x, axis, axis=0)
    held = x[None]
    masks = [0]
    for bit in bits[::-1]:
        pairs = [(q, q ^ bit) for q in range(count)]
        held = jnp.concatenate([held, lax.ppermute(held, axis, pairs)], axis=0)
        masks = masks + [m ^ bit for m in masks]
    inverse = [masks.index(m) for m in range(count)]
    table = jnp.array(inverse, jnp.int32)
    where = jnp.take(table, jnp.bitwise_xor(jnp.arange(count, dtype=jnp.int32), me))
    return jnp.take(held, where, axis=0)


def body(tokens, norm_gain, w_in, short_taps, rates, residues, w_out):
    tok_rows = tokens.shape[0]
    local_width = w_in.shape[2]
    local_groups = rates.shape[0]
    group_size = local_width // local_groups
    block_rows = BLOCK
    reach = block_rows - 1
    mode_count = rates.shape[1]
    highest = lax.Precision.HIGHEST
    n_ctx = lax.axis_size("ctx")
    n_grp = lax.axis_size("grp")
    me_ctx = lax.axis_index("ctx")
    me_grp = lax.axis_index("grp")
    shard_rows = w_in.shape[0]
    piece = shard_rows // n_grp
    streams = w_in.shape[1]

    span = short_taps.shape[0]
    halo = span - 1
    decay = rates[:, :, None]
    coef = residues * jnp.sqrt(-jnp.expm1(-2.0 * rates)) * mode_count ** (-0.5)
    lags = jnp.arange(block_rows).astype(jnp.float32)
    powers = jnp.exp(-decay * lags)
    long_taps = jnp.einsum("gn,gnt->gt", coef, powers, precision=highest)
    falling = coef[:, None, :] * jnp.exp(-rates[:, None, :] * lags[None, :, None])
    rising = jnp.exp(rates[:, None, :] * lags[None, :, None])
    square = jnp.einsum("gin,gjn->gij", falling, rising, precision=highest)
    kernel = jnp.where(lags[None, :, None] >= lags[None, None, :], square, 0.0)
    tail = jnp.exp(-decay * (reach - lags))
    entry = coef[:, None, :] * jnp.exp(-rates[:, None, :] * (lags[None, :, None] + 1.0))

    with_gain = jnp.concatenate([tokens, norm_gain[None]], axis=0)
    stacked = gather_by_swaps(with_gain, "tp")
    whole_rows = jnp.concatenate(list(stacked), axis=1)
    before = shifted(whole_rows[tok_rows - halo : tok_rows], "ctx", 1)
    gathered = jnp.concatenate([before, whole_rows], axis=0)
    own = lax.dynamic_slice_in_dim(w_in, me_grp * piece, piece, axis=0)

    def relay_send(got):
        doubled = jnp.concatenate([got, got], axis=0)
        return lax.dynamic_slice_in_dim(doubled, me_ctx + 1, n_ctx - 1, axis=0)

    def relay(send):
        received = []
        for by in range(1, n_grp):
            pairs = [(q, (q + by) % n_grp) for q in range(n_grp)]
            received.append(lax.ppermute(send, "grp", pairs))
        return received

    order = [0, 2, 1] if streams == 3 else list(range(streams))
    relayed = {}
    for s in order:
        got = lax.all_gather(own[:, s, :], "ctx", axis=0)
        if s == order[0]:
            got, kernel, tail, entry = lax.optimization_barrier((got, kernel, tail, entry))
        if s == order[-1] and len(order) > 1:
            relayed[s] = (got, None)
            continue
        send = relay_send(got)
        if s == order[0]:
            send, gathered = lax.optimization_barrier((send, gathered))
        relayed[s] = (got, relay(send))

    ext_rows = tok_rows + halo
    values = gathered[:ext_rows].astype(jnp.float32)
    gain_whole = gathered[ext_rows]
    scale = lax.rsqrt(jnp.mean(values * values, axis=1, keepdims=True) + 1e-06)
    normed = (values * scale * gain_whole.astype(jnp.float32)).astype(jnp.bfloat16)
    blocks = normed.reshape(ext_rows, n_ctx * n_grp, piece).transpose(1, 0, 2)
    shard_ids = jnp.arange(n_ctx, dtype=jnp.int32)
    mine = jnp.take(blocks, shard_ids * n_grp + me_grp, axis=0)
    others = []
    for by in range(1, n_grp):
        src_grp = (me_grp - by) % n_grp
        rolled = ((shard_ids + me_ctx) % n_ctx) * n_grp + src_grp
        others.append((src_grp, jnp.take(blocks, rolled, axis=0)))
    def project(s, received):
        got = relayed[s][0]
        acc = jnp.einsum("ktr,krc->tc", mine, got, preferred_element_type=jnp.float32)
        for (src_grp, part), recv in zip(others, received):
            local = lax.dynamic_slice_in_dim(w_in[:, s, :], src_grp * piece, piece, axis=0)
            acc = acc + jnp.dot(part[0], local, preferred_element_type=jnp.float32)
            acc = acc + jnp.einsum(
                "ktr,krc->tc", part[1:], recv, preferred_element_type=jnp.float32
            )
        rounded = lax.reduce_precision(acc, exponent_bits=8, mantissa_bits=7)
        return short_filter(rounded, short_taps[:, s, :], tok_rows)

    last = order[-1]
    filtered = {s: project(s, relayed[s][1]) for s in order[:-1]}
    first = order[0]
    if relayed[last][1] is None:
        filtered[first], tied = lax.optimization_barrier((filtered[first], relayed[last][0]))
        relayed[last] = (tied, relay(relay_send(tied)))
    product = filtered[0] * filtered[2]
    blocks = tok_rows // block_rows
    current = product.reshape(blocks, block_rows, local_groups, group_size)
    near = jnp.einsum("gij,bjgc->bigc", kernel, current, precision=highest)
    ends = jnp.einsum("gni,bigc->bgnc", tail, current, precision=highest)
    step_decay = jnp.exp(-decay * block_rows)

    def advance(state, end_block):
        return (step_decay * state + end_block, state)

    zero_state = jnp.zeros((local_groups, mode_count, group_size), jnp.float32)
    own_state, local_starts = lax.scan(advance, zero_state, ends)
    incoming = jnp.zeros_like(own_state)
    for by in range(1, n_ctx):
        pairs = [(k, k + by) for k in range(n_ctx - by)]
        arrived = lax.ppermute(own_state, "ctx", pairs)
        incoming = incoming + jnp.exp(-decay * (tok_rows * (by - 1.0))) * arrived
    block_index = jnp.arange(blocks).astype(jnp.float32)
    lead = jnp.exp(-decay[None] * block_rows * block_index[:, None, None, None])
    starts = lead * incoming[None] + local_starts
    distant = jnp.einsum("gin,bgnc->bigc", entry, starts, precision=highest)
    conv_out = (near + distant).reshape(tok_rows, local_width)
    late, conv_out = lax.optimization_barrier((relayed[last][1], conv_out))
    second = project(last, late)
    gated = (second * conv_out).astype(jnp.bfloat16)
    pieces = gather_by_swaps(gated, "tp")
    mixed = jnp.einsum("qtc,qcf->tf", pieces, w_out.reshape(pieces.shape[0], local_width, -1),
                       preferred_element_type=jnp.float32)
    return (tokens.astype(jnp.float32) + mixed).astype(jnp.bfloat16)


def solution(mesh):
    in_specs = (
        P(("grp", "ctx"), "tp"),
        P("tp"),
        P("ctx", None, "tp"),
        P(None, None, "tp"),
        P("tp", None),
        P("tp", None),
        P(None, "tp"),
    )
    out_specs = P(("grp", "ctx"), "tp")
    return jax.shard_map(body, mesh=mesh, in_specs=in_specs, out_specs=out_specs, check_vma=False)
```

```python
import jax
import jax.numpy as jnp
from jax import lax
from jax.sharding import PartitionSpec as P

BLOCK = 128


def shifted(x, axis, by):
    count = lax.axis_size(axis)
    pairs = [(i, i + by) for i in range(count) if 0 <= i + by < count]
    return lax.ppermute(x, axis, pairs)


def short_filter(extended, taps, count):
    values = extended.astype(jnp.float32)
    result = jnp.zeros((count, values.shape[1]), jnp.float32)
    span = taps.shape[0]
    for tap_index in range(span):
        begin = span - 1 - tap_index
        result = result + taps[tap_index] * values[begin : begin + count]
    return result


def banded(series):
    group_count, length = series.shape
    padded = jnp.concatenate([series, jnp.zeros_like(series)], axis=1)
    tiled = jnp.tile(padded, (1, length))
    return tiled[:, : length * (2 * length - 1)].reshape(group_count, length, 2 * length - 1)


def gather_by_permutes(x, axis):
    count = lax.axis_size(axis)
    me = lax.axis_index(axis)
    pieces = [x]
    for by in range(1, count):
        pairs = [(s, (s + by) % count) for s in range(count)]
        pieces.append(lax.ppermute(x, axis, pairs))
    stacked = jnp.stack(pieces[::-1], axis=0)
    return jnp.roll(stacked, me + 1, axis=0)


def gather_by_swaps(x, axis):
    count = lax.axis_size(axis)
    me = lax.axis_index(axis)
    bits = []
    b = 1
    while b < count:
        bits.append(b)
        b *= 2
    if 2 ** len(bits) != count:
        return lax.all_gather(x, axis, axis=0)
    held = x[None]
    masks = [0]
    for bit in bits[::-1]:
        pairs = [(q, q ^ bit) for q in range(count)]
        held = jnp.concatenate([held, lax.ppermute(held, axis, pairs)], axis=0)
        masks = masks + [m ^ bit for m in masks]
    inverse = [masks.index(m) for m in range(count)]
    table = jnp.array(inverse, jnp.int32)
    where = jnp.take(table, jnp.bitwise_xor(jnp.arange(count, dtype=jnp.int32), me))
    return jnp.take(held, where, axis=0)


def body(tokens, norm_gain, w_in, short_taps, rates, residues, w_out):
    tok_rows = tokens.shape[0]
    local_width = w_in.shape[2]
    local_groups = rates.shape[0]
    group_size = local_width // local_groups
    block_rows = BLOCK
    reach = block_rows - 1
    mode_count = rates.shape[1]
    highest = lax.Precision.HIGHEST
    n_ctx = lax.axis_size("ctx")
    n_grp = lax.axis_size("grp")
    me_ctx = lax.axis_index("ctx")
    me_grp = lax.axis_index("grp")
    shard_rows = w_in.shape[0]
    piece = shard_rows // n_grp
    streams = w_in.shape[1]

    span = short_taps.shape[0]
    halo = span - 1
    decay = rates[:, :, None]
    coef = residues * jnp.sqrt(-jnp.expm1(-2.0 * rates)) * mode_count ** (-0.5)
    lags = jnp.arange(block_rows).astype(jnp.float32)
    powers = jnp.exp(-decay * lags)
    long_taps = jnp.einsum("gn,gnt->gt", coef, powers, precision=highest)
    falling = coef[:, None, :] * jnp.exp(-rates[:, None, :] * lags[None, :, None])
    rising = jnp.exp(rates[:, None, :] * lags[None, :, None])
    square = jnp.einsum("gin,gjn->gij", falling, rising, precision=highest)
    kernel = jnp.where(lags[None, :, None] >= lags[None, None, :], square, 0.0)
    tail = jnp.exp(-decay * (reach - lags))
    entry = coef[:, None, :] * jnp.exp(-rates[:, None, :] * (lags[None, :, None] + 1.0))

    with_gain = jnp.concatenate([tokens, norm_gain[None]], axis=0)
    stacked = gather_by_swaps(with_gain, "tp")
    whole_rows = jnp.concatenate(list(stacked), axis=1)
    before = shifted(whole_rows[tok_rows - halo : tok_rows], "ctx", 1)
    gathered = jnp.concatenate([before, whole_rows], axis=0)
    own = lax.dynamic_slice_in_dim(w_in, me_grp * piece, piece, axis=0)

    def relay_send(got):
        return got[1:]

    def gather_ctx(piece_arr):
        if n_ctx > 8:
            got = lax.all_gather(piece_arr, "ctx", axis=0)
            doubled = jnp.concatenate([got, got], axis=0)
            return lax.dynamic_slice_in_dim(doubled, me_ctx, n_ctx, axis=0)
        rights, lefts = [], []
        to_right, to_left = piece_arr, piece_arr
        for _ in range(1, n_ctx):
            to_right = lax.ppermute(to_right, "ctx", [(k, k + 1) for k in range(n_ctx - 1)])
            to_left = lax.ppermute(to_left, "ctx", [(k + 1, k) for k in range(n_ctx - 1)])
            rights.append(to_right)
            lefts.append(to_left)
        rolled = [piece_arr]
        for m in range(1, n_ctx):
            rolled.append(jnp.where(me_ctx + m < n_ctx, lefts[m - 1], rights[n_ctx - m - 1]))
        return jnp.stack(rolled, axis=0)

    def relay(send):
        received = []
        for by in range(1, n_grp):
            pairs = [(q, (q + by) % n_grp) for q in range(n_grp)]
            received.append(lax.ppermute(send, "grp", pairs))
        return received

    order = [0, 2, 1] if streams == 3 else list(range(streams))
    relayed = {}
    for s in order:
        got = gather_ctx(own[:, s, :])
        if s == order[0]:
            got, kernel, tail, entry = lax.optimization_barrier((got, kernel, tail, entry))
        if s == order[-1] and len(order) > 1:
            relayed[s] = (got, None)
            continue
        send = relay_send(got)
        if s == order[0]:
            send, gathered = lax.optimization_barrier((send, gathered))
        relayed[s] = (got, relay(send))

    ext_rows = tok_rows + halo
    values = gathered[:ext_rows].astype(jnp.float32)
    gain_whole = gathered[ext_rows]
    scale = lax.rsqrt(jnp.mean(values * values, axis=1, keepdims=True) + 1e-06)
    normed = (values * scale * gain_whole.astype(jnp.float32)).astype(jnp.bfloat16)
    blocks = normed.reshape(ext_rows, n_ctx * n_grp, piece).transpose(1, 0, 2)
    shard_ids = jnp.arange(n_ctx, dtype=jnp.int32)
    mine = jnp.take(blocks, ((shard_ids + me_ctx) % n_ctx) * n_grp + me_grp, axis=0)
    others = []
    for by in range(1, n_grp):
        src_grp = (me_grp - by) % n_grp
        rolled = ((shard_ids + me_ctx) % n_ctx) * n_grp + src_grp
        others.append((src_grp, jnp.take(blocks, rolled, axis=0)))
    def project(s, received):
        got = relayed[s][0]
        acc = jnp.einsum("ktr,krc->tc", mine, got, preferred_element_type=jnp.float32)
        for (src_grp, part), recv in zip(others, received):
            local = lax.dynamic_slice_in_dim(w_in[:, s, :], src_grp * piece, piece, axis=0)
            acc = acc + jnp.dot(part[0], local, preferred_element_type=jnp.float32)
            acc = acc + jnp.einsum(
                "ktr,krc->tc", part[1:], recv, preferred_element_type=jnp.float32
            )
        rounded = lax.reduce_precision(acc, exponent_bits=8, mantissa_bits=7)
        return short_filter(rounded, short_taps[:, s, :], tok_rows)

    last = order[-1]
    filtered = {s: project(s, relayed[s][1]) for s in order[:-1]}
    first = order[0]
    if relayed[last][1] is None:
        filtered[first], tied = lax.optimization_barrier((filtered[first], relayed[last][0]))
        relayed[last] = (tied, relay(relay_send(tied)))
    product = filtered[0] * filtered[2]
    blocks = tok_rows // block_rows
    current = product.reshape(blocks, block_rows, local_groups, group_size)
    near = jnp.einsum("gij,bjgc->bigc", kernel, current, precision=highest)
    ends = jnp.einsum("gni,bigc->bgnc", tail, current, precision=highest)
    step_decay = jnp.exp(-decay * block_rows)

    def advance(state, end_block):
        return (step_decay * state + end_block, state)

    zero_state = jnp.zeros((local_groups, mode_count, group_size), jnp.float32)
    own_state, local_starts = lax.scan(advance, zero_state, ends)
    incoming = jnp.zeros_like(own_state)
    for by in range(1, n_ctx):
        pairs = [(k, k + by) for k in range(n_ctx - by)]
        arrived = lax.ppermute(own_state, "ctx", pairs)
        incoming = incoming + jnp.exp(-decay * (tok_rows * (by - 1.0))) * arrived
    block_index = jnp.arange(blocks).astype(jnp.float32)
    lead = jnp.exp(-decay[None] * block_rows * block_index[:, None, None, None])
    starts = lead * incoming[None] + local_starts
    distant = jnp.einsum("gin,bgnc->bigc", entry, starts, precision=highest)
    conv_out = (near + distant).reshape(tok_rows, local_width)
    late, conv_out = lax.optimization_barrier((relayed[last][1], conv_out))
    second = project(last, late)
    gated = (second * conv_out).astype(jnp.bfloat16)
    pieces = gather_by_swaps(gated, "tp")
    mixed = jnp.einsum("qtc,qcf->tf", pieces, w_out.reshape(pieces.shape[0], local_width, -1),
                       preferred_element_type=jnp.float32)
    return (tokens.astype(jnp.float32) + mixed).astype(jnp.bfloat16)


def solution(mesh):
    in_specs = (
        P(("grp", "ctx"), "tp"),
        P("tp"),
        P("ctx", None, "tp"),
        P(None, None, "tp"),
        P("tp", None),
        P("tp", None),
        P(None, "tp"),
    )
    out_specs = P(("grp", "ctx"), "tp")
    return jax.shard_map(body, mesh=mesh, in_specs=in_specs, out_specs=out_specs, check_vma=False)
```

```python
import jax
import jax.numpy as jnp
from jax import lax
from jax.sharding import PartitionSpec as P

BLOCK = 128


def shifted(x, axis, by):
    count = lax.axis_size(axis)
    pairs = [(i, i + by) for i in range(count) if 0 <= i + by < count]
    return lax.ppermute(x, axis, pairs)


def short_filter(extended, taps, count):
    values = extended.astype(jnp.float32)
    result = jnp.zeros((count, values.shape[1]), jnp.float32)
    span = taps.shape[0]
    for tap_index in range(span):
        begin = span - 1 - tap_index
        result = result + taps[tap_index] * values[begin : begin + count]
    return result


def banded(series):
    group_count, length = series.shape
    padded = jnp.concatenate([series, jnp.zeros_like(series)], axis=1)
    tiled = jnp.tile(padded, (1, length))
    return tiled[:, : length * (2 * length - 1)].reshape(group_count, length, 2 * length - 1)


def gather_by_permutes(x, axis):
    count = lax.axis_size(axis)
    me = lax.axis_index(axis)
    pieces = [x]
    for by in range(1, count):
        pairs = [(s, (s + by) % count) for s in range(count)]
        pieces.append(lax.ppermute(x, axis, pairs))
    stacked = jnp.stack(pieces[::-1], axis=0)
    return jnp.roll(stacked, me + 1, axis=0)


def gather_by_swaps(x, axis):
    count = lax.axis_size(axis)
    me = lax.axis_index(axis)
    bits = []
    b = 1
    while b < count:
        bits.append(b)
        b *= 2
    if 2 ** len(bits) != count:
        return lax.all_gather(x, axis, axis=0)
    held = x[None]
    masks = [0]
    for bit in bits[::-1]:
        pairs = [(q, q ^ bit) for q in range(count)]
        held = jnp.concatenate([held, lax.ppermute(held, axis, pairs)], axis=0)
        masks = masks + [m ^ bit for m in masks]
    inverse = [masks.index(m) for m in range(count)]
    table = jnp.array(inverse, jnp.int32)
    where = jnp.take(table, jnp.bitwise_xor(jnp.arange(count, dtype=jnp.int32), me))
    return jnp.take(held, where, axis=0)


def body(tokens, norm_gain, w_in, short_taps, rates, residues, w_out):
    tok_rows = tokens.shape[0]
    local_width = w_in.shape[2]
    local_groups = rates.shape[0]
    group_size = local_width // local_groups
    block_rows = BLOCK
    reach = block_rows - 1
    mode_count = rates.shape[1]
    highest = lax.Precision.HIGHEST
    n_ctx = lax.axis_size("ctx")
    n_grp = lax.axis_size("grp")
    me_ctx = lax.axis_index("ctx")
    me_grp = lax.axis_index("grp")
    shard_rows = w_in.shape[0]
    piece = shard_rows // n_grp
    streams = w_in.shape[1]

    span = short_taps.shape[0]
    halo = span - 1
    decay = rates[:, :, None]
    coef = residues * jnp.sqrt(-jnp.expm1(-2.0 * rates)) * mode_count ** (-0.5)
    lags = jnp.arange(block_rows).astype(jnp.float32)
    powers = jnp.exp(-decay * lags)
    long_taps = jnp.einsum("gn,gnt->gt", coef, powers, precision=highest)
    falling = coef[:, None, :] * jnp.exp(-rates[:, None, :] * lags[None, :, None])
    rising = jnp.exp(rates[:, None, :] * lags[None, :, None])
    square = jnp.einsum("gin,gjn->gij", falling, rising, precision=highest)
    kernel = jnp.where(lags[None, :, None] >= lags[None, None, :], square, 0.0)
    tail = jnp.exp(-decay * (reach - lags))
    entry = coef[:, None, :] * jnp.exp(-rates[:, None, :] * (lags[None, :, None] + 1.0))

    with_gain = jnp.concatenate([tokens, norm_gain[None]], axis=0)
    stacked = gather_by_swaps(with_gain, "tp")
    whole_rows = jnp.concatenate(list(stacked), axis=1)
    before = shifted(whole_rows[tok_rows - halo : tok_rows], "ctx", 1)
    gathered = jnp.concatenate([before, whole_rows], axis=0)
    own = lax.dynamic_slice_in_dim(w_in, me_grp * piece, piece, axis=0)

    def relay_send(got):
        doubled = jnp.concatenate([got, got], axis=0)
        return lax.dynamic_slice_in_dim(doubled, me_ctx + 1, n_ctx - 1, axis=0)

    def relay(send):
        received = []
        for by in range(1, n_grp):
            pairs = [(q, (q + by) % n_grp) for q in range(n_grp)]
            received.append(lax.ppermute(send, "grp", pairs))
        return received

    order = [0, 2, 1] if streams == 3 else list(range(streams))
    relayed = {}
    for s in order:
        got = lax.all_gather(own[:, s, :], "ctx", axis=0)
        if s == order[0]:
            got, kernel, tail, entry = lax.optimization_barrier((got, kernel, tail, entry))
        if s == order[-1] and len(order) > 1:
            relayed[s] = (got, None)
            continue
        send = relay_send(got)
        if s == order[0]:
            send, gathered = lax.optimization_barrier((send, gathered))
        relayed[s] = (got, relay(send))

    ext_rows = tok_rows + halo
    values = gathered[:ext_rows].astype(jnp.float32)
    gain_whole = gathered[ext_rows]
    scale = lax.rsqrt(jnp.mean(values * values, axis=1, keepdims=True) + 1e-06)
    normed = (values * scale * gain_whole.astype(jnp.float32)).astype(jnp.bfloat16)
    blocks = normed.reshape(ext_rows, n_ctx * n_grp, piece).transpose(1, 0, 2)
    shard_ids = jnp.arange(n_ctx, dtype=jnp.int32)
    mine = jnp.take(blocks, shard_ids * n_grp + me_grp, axis=0)
    others = []
    for by in range(1, n_grp):
        src_grp = (me_grp - by) % n_grp
        rolled = ((shard_ids + me_ctx) % n_ctx) * n_grp + src_grp
        others.append((src_grp, jnp.take(blocks, rolled, axis=0)))
    def project(s, received):
        got = relayed[s][0]
        acc = jnp.einsum("ktr,krc->tc", mine, got, preferred_element_type=jnp.float32)
        for (src_grp, part), recv in zip(others, received):
            local = lax.dynamic_slice_in_dim(w_in[:, s, :], src_grp * piece, piece, axis=0)
            acc = acc + jnp.dot(part[0], local, preferred_element_type=jnp.float32)
            acc = acc + jnp.einsum(
                "ktr,krc->tc", part[1:], recv, preferred_element_type=jnp.float32
            )
        rounded = lax.reduce_precision(acc, exponent_bits=8, mantissa_bits=7)
        return short_filter(rounded, short_taps[:, s, :], tok_rows)

    last = order[-1]
    filtered = {s: project(s, relayed[s][1]) for s in order[:-1]}
    first = order[0]
    if relayed[last][1] is None:
        filtered[first], tied = lax.optimization_barrier((filtered[first], relayed[last][0]))
        relayed[last] = (tied, relay(relay_send(tied)))
    product = filtered[0] * filtered[2]
    blocks = tok_rows // block_rows
    current = product.reshape(blocks, block_rows, local_groups, group_size)
    near = jnp.einsum("gij,bjgc->bigc", kernel, current, precision=highest)
    ends = jnp.einsum("gni,bigc->bgnc", tail, current, precision=highest)
    step_decay = jnp.exp(-decay * block_rows)

    def advance(state, end_block):
        return (step_decay * state + end_block, state)

    zero_state = jnp.zeros((local_groups, mode_count, group_size), jnp.float32)
    own_state, local_starts = lax.scan(advance, zero_state, ends)
    incoming = jnp.zeros_like(own_state)
    for by in range(1, n_ctx):
        pairs = [(k, k + by) for k in range(n_ctx - by)]
        arrived = lax.ppermute(own_state, "ctx", pairs)
        incoming = incoming + jnp.exp(-decay * (tok_rows * (by - 1.0))) * arrived
    block_index = jnp.arange(blocks).astype(jnp.float32)
    lead = jnp.exp(-decay[None] * block_rows * block_index[:, None, None, None])
    starts = lead * incoming[None] + local_starts
    distant = jnp.einsum("gin,bgnc->bigc", entry, starts, precision=highest)
    conv_out = (near + distant).reshape(tok_rows, local_width)
    late, conv_out = lax.optimization_barrier((relayed[last][1], conv_out))
    second = project(last, late)
    gated = (second * conv_out).astype(jnp.bfloat16)
    count = lax.axis_size("tp")
    me_tp = lax.axis_index("tp")

    def contribution(block, source):
        rows = lax.dynamic_slice_in_dim(w_out, source * local_width, local_width, axis=0)
        return jnp.dot(block, rows, preferred_element_type=jnp.float32)

    if count & (count - 1) == 0:
        mixed = contribution(gated, me_tp)
        held = gated[None]
        masks = [0]
        bit = count // 2
        while bit >= 1:
            pairs = [(q, q ^ bit) for q in range(count)]
            arrived = lax.ppermute(held, "tp", pairs)
            for q, m in enumerate(masks):
                mixed = mixed + contribution(arrived[q], jnp.bitwise_xor(me_tp, m ^ bit))
            held = jnp.concatenate([held, arrived], axis=0)
            masks = masks + [m ^ bit for m in masks]
            bit //= 2
    else:
        pieces = gather_by_swaps(gated, "tp")
        mixed = jnp.einsum("qtc,qcf->tf", pieces, w_out.reshape(pieces.shape[0], local_width, -1),
                           preferred_element_type=jnp.float32)
    return (tokens.astype(jnp.float32) + mixed).astype(jnp.bfloat16)


def solution(mesh):
    in_specs = (
        P(("grp", "ctx"), "tp"),
        P("tp"),
        P("ctx", None, "tp"),
        P(None, None, "tp"),
        P("tp", None),
        P("tp", None),
        P(None, "tp"),
    )
    out_specs = P(("grp", "ctx"), "tp")
    return jax.shard_map(body, mesh=mesh, in_specs=in_specs, out_specs=out_specs, check_vma=False)
```

```python
import jax
import jax.numpy as jnp
from jax import lax
from jax.sharding import PartitionSpec as P

BLOCK = 128


def shifted(x, axis, by):
    count = lax.axis_size(axis)
    pairs = [(i, i + by) for i in range(count) if 0 <= i + by < count]
    return lax.ppermute(x, axis, pairs)


def short_filter(extended, taps, count):
    values = extended.astype(jnp.float32)
    result = jnp.zeros((count, values.shape[1]), jnp.float32)
    span = taps.shape[0]
    for tap_index in range(span):
        begin = span - 1 - tap_index
        result = result + taps[tap_index] * values[begin : begin + count]
    return result


def banded(series):
    group_count, length = series.shape
    padded = jnp.concatenate([series, jnp.zeros_like(series)], axis=1)
    tiled = jnp.tile(padded, (1, length))
    return tiled[:, : length * (2 * length - 1)].reshape(group_count, length, 2 * length - 1)


def gather_by_permutes(x, axis):
    count = lax.axis_size(axis)
    me = lax.axis_index(axis)
    pieces = [x]
    for by in range(1, count):
        pairs = [(s, (s + by) % count) for s in range(count)]
        pieces.append(lax.ppermute(x, axis, pairs))
    stacked = jnp.stack(pieces[::-1], axis=0)
    return jnp.roll(stacked, me + 1, axis=0)


def gather_by_swaps(x, axis):
    count = lax.axis_size(axis)
    me = lax.axis_index(axis)
    bits = []
    b = 1
    while b < count:
        bits.append(b)
        b *= 2
    if 2 ** len(bits) != count:
        return lax.all_gather(x, axis, axis=0)
    held = x[None]
    masks = [0]
    for bit in bits[::-1]:
        pairs = [(q, q ^ bit) for q in range(count)]
        held = jnp.concatenate([held, lax.ppermute(held, axis, pairs)], axis=0)
        masks = masks + [m ^ bit for m in masks]
    inverse = [masks.index(m) for m in range(count)]
    table = jnp.array(inverse, jnp.int32)
    where = jnp.take(table, jnp.bitwise_xor(jnp.arange(count, dtype=jnp.int32), me))
    return jnp.take(held, where, axis=0)


def body(tokens, norm_gain, w_in, short_taps, rates, residues, w_out):
    tok_rows = tokens.shape[0]
    local_width = w_in.shape[2]
    local_groups = rates.shape[0]
    group_size = local_width // local_groups
    block_rows = BLOCK
    reach = block_rows - 1
    mode_count = rates.shape[1]
    highest = lax.Precision.HIGHEST
    n_ctx = lax.axis_size("ctx")
    n_grp = lax.axis_size("grp")
    me_ctx = lax.axis_index("ctx")
    me_grp = lax.axis_index("grp")
    shard_rows = w_in.shape[0]
    piece = shard_rows // n_grp
    streams = w_in.shape[1]

    span = short_taps.shape[0]
    halo = span - 1
    decay = rates[:, :, None]
    coef = residues * jnp.sqrt(-jnp.expm1(-2.0 * rates)) * mode_count ** (-0.5)
    lags = jnp.arange(block_rows).astype(jnp.float32)
    powers = jnp.exp(-decay * lags)
    long_taps = jnp.einsum("gn,gnt->gt", coef, powers, precision=highest)
    falling = coef[:, None, :] * jnp.exp(-rates[:, None, :] * lags[None, :, None])
    rising = jnp.exp(rates[:, None, :] * lags[None, :, None])
    square = jnp.einsum("gin,gjn->gij", falling, rising, precision=highest)
    kernel = jnp.where(lags[None, :, None] >= lags[None, None, :], square, 0.0)
    tail = jnp.exp(-decay * (reach - lags))
    entry = coef[:, None, :] * jnp.exp(-rates[:, None, :] * (lags[None, :, None] + 1.0))

    with_gain = jnp.concatenate([tokens, norm_gain[None]], axis=0)
    stacked = gather_by_swaps(with_gain, "tp")
    whole_rows = jnp.concatenate(list(stacked), axis=1)
    before = shifted(whole_rows[tok_rows - halo : tok_rows], "ctx", 1)
    gathered = jnp.concatenate([before, whole_rows], axis=0)
    own = lax.dynamic_slice_in_dim(w_in, me_grp * piece, piece, axis=0)

    def relay_send(got):
        doubled = jnp.concatenate([got, got], axis=0)
        return lax.dynamic_slice_in_dim(doubled, me_ctx + 1, n_ctx - 1, axis=0)

    def relay(send):
        received = []
        for by in range(1, n_grp):
            pairs = [(q, (q + by) % n_grp) for q in range(n_grp)]
            received.append(lax.ppermute(send, "grp", pairs))
        return received

    stream_order = [0, 2, 1] if streams == 3 else list(range(streams))
    width = streams * local_width
    own_cat = jnp.concatenate([own[:, s, :] for s in stream_order], axis=1)
    w_cat = jnp.concatenate([w_in[:, s, :] for s in stream_order], axis=1)
    taps_cat = jnp.concatenate([short_taps[:, s, :] for s in stream_order], axis=1)
    if streams == 3:
        cuts = [0, 5 * width // 12, 10 * width // 12, width]
    else:
        cuts = [s * local_width for s in range(streams + 1)]
    order = [(cuts[c], cuts[c + 1]) for c in range(len(cuts) - 1)]
    relayed = {}
    previous = None
    for index, chunk in enumerate(order):
        lo, hi = chunk
        operand = own_cat[:, lo:hi]
        if index >= 2:
            operand, _ = lax.optimization_barrier((operand, previous))
        got = lax.all_gather(operand, "ctx", axis=0)
        previous = got
        if index == 0:
            got, kernel, tail, entry = lax.optimization_barrier((got, kernel, tail, entry))
        if chunk == order[-1] and len(order) > 1:
            relayed[chunk] = (got, None)
            continue
        send = relay_send(got)
        if index == 0:
            send, gathered = lax.optimization_barrier((send, gathered))
        relayed[chunk] = (got, relay(send))

    ext_rows = tok_rows + halo
    values = gathered[:ext_rows].astype(jnp.float32)
    gain_whole = gathered[ext_rows]
    scale = lax.rsqrt(jnp.mean(values * values, axis=1, keepdims=True) + 1e-06)
    normed = (values * scale * gain_whole.astype(jnp.float32)).astype(jnp.bfloat16)
    blocks = normed.reshape(ext_rows, n_ctx * n_grp, piece).transpose(1, 0, 2)
    shard_ids = jnp.arange(n_ctx, dtype=jnp.int32)
    mine = jnp.take(blocks, shard_ids * n_grp + me_grp, axis=0)
    others = []
    for by in range(1, n_grp):
        src_grp = (me_grp - by) % n_grp
        rolled = ((shard_ids + me_ctx) % n_ctx) * n_grp + src_grp
        others.append((src_grp, jnp.take(blocks, rolled, axis=0)))
    def project(chunk, received):
        lo, hi = chunk
        got = relayed[chunk][0]
        acc = jnp.einsum("ktr,krc->tc", mine, got, preferred_element_type=jnp.float32)
        for (src_grp, part), recv in zip(others, received):
            local = lax.dynamic_slice_in_dim(w_cat[:, lo:hi], src_grp * piece, piece, axis=0)
            acc = acc + jnp.dot(part[0], local, preferred_element_type=jnp.float32)
            acc = acc + jnp.einsum(
                "ktr,krc->tc", part[1:], recv, preferred_element_type=jnp.float32
            )
        rounded = lax.reduce_precision(acc, exponent_bits=8, mantissa_bits=7)
        return short_filter(rounded, taps_cat[:, lo:hi], tok_rows)

    last = order[-1]
    filtered = {chunk: project(chunk, relayed[chunk][1]) for chunk in order[:-1]}
    first = order[0]
    if relayed[last][1] is None:
        filtered[first], tied = lax.optimization_barrier((filtered[first], relayed[last][0]))
        relayed[last] = (tied, relay(relay_send(tied)))
    early = jnp.concatenate([filtered[c] for c in order[:-1]], axis=1)
    product = early[:, :local_width] * early[:, local_width : 2 * local_width]
    blocks = tok_rows // block_rows
    current = product.reshape(blocks, block_rows, local_groups, group_size)
    near = jnp.einsum("gij,bjgc->bigc", kernel, current, precision=highest)
    ends = jnp.einsum("gni,bigc->bgnc", tail, current, precision=highest)
    step_decay = jnp.exp(-decay * block_rows)

    def advance(state, end_block):
        return (step_decay * state + end_block, state)

    zero_state = jnp.zeros((local_groups, mode_count, group_size), jnp.float32)
    own_state, local_starts = lax.scan(advance, zero_state, ends)
    incoming = jnp.zeros_like(own_state)
    for by in range(1, n_ctx):
        pairs = [(k, k + by) for k in range(n_ctx - by)]
        arrived = lax.ppermute(own_state, "ctx", pairs)
        incoming = incoming + jnp.exp(-decay * (tok_rows * (by - 1.0))) * arrived
    block_index = jnp.arange(blocks).astype(jnp.float32)
    lead = jnp.exp(-decay[None] * block_rows * block_index[:, None, None, None])
    starts = lead * incoming[None] + local_starts
    distant = jnp.einsum("gin,bgnc->bigc", entry, starts, precision=highest)
    conv_out = (near + distant).reshape(tok_rows, local_width)
    late, conv_out = lax.optimization_barrier((relayed[last][1], conv_out))
    late_part = project(last, late)
    second = jnp.concatenate([early[:, 2 * local_width :], late_part], axis=1)
    gated = (second * conv_out).astype(jnp.bfloat16)
    count = lax.axis_size("tp")
    me_tp = lax.axis_index("tp")

    def contribution(block, source):
        rows = lax.dynamic_slice_in_dim(w_out, source * local_width, local_width, axis=0)
        return jnp.dot(block, rows, preferred_element_type=jnp.float32)

    if count & (count - 1) == 0:
        mixed = contribution(gated, me_tp)
        held = gated[None]
        masks = [0]
        bit = count // 2
        while bit >= 1:
            pairs = [(q, q ^ bit) for q in range(count)]
            arrived = lax.ppermute(held, "tp", pairs)
            for q, m in enumerate(masks):
                mixed = mixed + contribution(arrived[q], jnp.bitwise_xor(me_tp, m ^ bit))
            held = jnp.concatenate([held, arrived], axis=0)
            masks = masks + [m ^ bit for m in masks]
            bit //= 2
    else:
        pieces = gather_by_swaps(gated, "tp")
        mixed = jnp.einsum("qtc,qcf->tf", pieces, w_out.reshape(pieces.shape[0], local_width, -1),
                           preferred_element_type=jnp.float32)
    return (tokens.astype(jnp.float32) + mixed).astype(jnp.bfloat16)


def solution(mesh):
    in_specs = (
        P(("grp", "ctx"), "tp"),
        P("tp"),
        P("ctx", None, "tp"),
        P(None, None, "tp"),
        P("tp", None),
        P("tp", None),
        P(None, "tp"),
    )
    out_specs = P(("grp", "ctx"), "tp")
    return jax.shard_map(body, mesh=mesh, in_specs=in_specs, out_specs=out_specs, check_vma=False)
```

```python
import jax
import jax.numpy as jnp
from jax import lax
from jax.sharding import PartitionSpec as P

BLOCK = 128


def shifted(x, axis, by):
    count = lax.axis_size(axis)
    pairs = [(i, i + by) for i in range(count) if 0 <= i + by < count]
    return lax.ppermute(x, axis, pairs)


def short_filter(extended, taps, count):
    values = extended.astype(jnp.float32)
    result = jnp.zeros((count, values.shape[1]), jnp.float32)
    span = taps.shape[0]
    for tap_index in range(span):
        begin = span - 1 - tap_index
        result = result + taps[tap_index] * values[begin : begin + count]
    return result


def banded(series):
    group_count, length = series.shape
    padded = jnp.concatenate([series, jnp.zeros_like(series)], axis=1)
    tiled = jnp.tile(padded, (1, length))
    return tiled[:, : length * (2 * length - 1)].reshape(group_count, length, 2 * length - 1)


def gather_by_permutes(x, axis):
    count = lax.axis_size(axis)
    me = lax.axis_index(axis)
    pieces = [x]
    for by in range(1, count):
        pairs = [(s, (s + by) % count) for s in range(count)]
        pieces.append(lax.ppermute(x, axis, pairs))
    stacked = jnp.stack(pieces[::-1], axis=0)
    return jnp.roll(stacked, me + 1, axis=0)


def gather_by_swaps(x, axis):
    count = lax.axis_size(axis)
    me = lax.axis_index(axis)
    bits = []
    b = 1
    while b < count:
        bits.append(b)
        b *= 2
    if 2 ** len(bits) != count:
        return lax.all_gather(x, axis, axis=0)
    held = x[None]
    masks = [0]
    for bit in bits[::-1]:
        pairs = [(q, q ^ bit) for q in range(count)]
        held = jnp.concatenate([held, lax.ppermute(held, axis, pairs)], axis=0)
        masks = masks + [m ^ bit for m in masks]
    inverse = [masks.index(m) for m in range(count)]
    table = jnp.array(inverse, jnp.int32)
    where = jnp.take(table, jnp.bitwise_xor(jnp.arange(count, dtype=jnp.int32), me))
    return jnp.take(held, where, axis=0)


def body(tokens, norm_gain, w_in, short_taps, rates, residues, w_out):
    tok_rows = tokens.shape[0]
    local_width = w_in.shape[2]
    local_groups = rates.shape[0]
    group_size = local_width // local_groups
    block_rows = BLOCK
    reach = block_rows - 1
    mode_count = rates.shape[1]
    highest = lax.Precision.HIGHEST
    n_ctx = lax.axis_size("ctx")
    n_grp = lax.axis_size("grp")
    me_ctx = lax.axis_index("ctx")
    me_grp = lax.axis_index("grp")
    shard_rows = w_in.shape[0]
    piece = shard_rows // n_grp
    streams = w_in.shape[1]

    span = short_taps.shape[0]
    halo = span - 1
    decay = rates[:, :, None]
    coef = residues * jnp.sqrt(-jnp.expm1(-2.0 * rates)) * mode_count ** (-0.5)
    lags = jnp.arange(block_rows).astype(jnp.float32)
    powers = jnp.exp(-decay * lags)
    long_taps = jnp.einsum("gn,gnt->gt", coef, powers, precision=highest)
    falling = coef[:, None, :] * jnp.exp(-rates[:, None, :] * lags[None, :, None])
    rising = jnp.exp(rates[:, None, :] * lags[None, :, None])
    square = jnp.einsum("gin,gjn->gij", falling, rising, precision=highest)
    kernel = jnp.where(lags[None, :, None] >= lags[None, None, :], square, 0.0)
    tail = jnp.exp(-decay * (reach - lags))
    entry = coef[:, None, :] * jnp.exp(-rates[:, None, :] * (lags[None, :, None] + 1.0))

    with_gain = jnp.concatenate([tokens, norm_gain[None]], axis=0)
    stacked = gather_by_swaps(with_gain, "tp")
    whole_rows = jnp.concatenate(list(stacked), axis=1)
    before = shifted(whole_rows[tok_rows - halo : tok_rows], "ctx", 1)
    gathered = jnp.concatenate([before, whole_rows], axis=0)
    own = lax.dynamic_slice_in_dim(w_in, me_grp * piece, piece, axis=0)

    def relay_send(got):
        doubled = jnp.concatenate([got, got], axis=0)
        return lax.dynamic_slice_in_dim(doubled, me_ctx + 1, n_ctx - 1, axis=0)

    def relay(send):
        received = []
        for by in range(1, n_grp):
            pairs = [(q, (q + by) % n_grp) for q in range(n_grp)]
            received.append(lax.ppermute(send, "grp", pairs))
        return received

    order = [0, 2, 1] if streams == 3 else list(range(streams))
    relayed = {}
    previous = None
    for s in order:
        if s == order[-1] and len(order) > 1:
            operand, _ = lax.optimization_barrier((w_in[:, s, :], previous))
            relayed[s] = (lax.all_gather(operand, "ctx", axis=0, tiled=True), None)
            continue
        got = lax.all_gather(own[:, s, :], "ctx", axis=0)
        previous = got
        if s == order[0]:
            got, kernel, tail, entry = lax.optimization_barrier((got, kernel, tail, entry))
        send = relay_send(got)
        if s == order[0]:
            send, gathered = lax.optimization_barrier((send, gathered))
        relayed[s] = (got, relay(send))

    ext_rows = tok_rows + halo
    values = gathered[:ext_rows].astype(jnp.float32)
    gain_whole = gathered[ext_rows]
    scale = lax.rsqrt(jnp.mean(values * values, axis=1, keepdims=True) + 1e-06)
    normed = (values * scale * gain_whole.astype(jnp.float32)).astype(jnp.bfloat16)
    blocks = normed.reshape(ext_rows, n_ctx * n_grp, piece).transpose(1, 0, 2)
    shard_ids = jnp.arange(n_ctx, dtype=jnp.int32)
    mine = jnp.take(blocks, shard_ids * n_grp + me_grp, axis=0)
    others = []
    for by in range(1, n_grp):
        src_grp = (me_grp - by) % n_grp
        rolled = ((shard_ids + me_ctx) % n_ctx) * n_grp + src_grp
        others.append((src_grp, jnp.take(blocks, rolled, axis=0)))
    def project(s, received):
        got = relayed[s][0]
        acc = jnp.einsum("ktr,krc->tc", mine, got, preferred_element_type=jnp.float32)
        for (src_grp, part), recv in zip(others, received):
            local = lax.dynamic_slice_in_dim(w_in[:, s, :], src_grp * piece, piece, axis=0)
            acc = acc + jnp.dot(part[0], local, preferred_element_type=jnp.float32)
            acc = acc + jnp.einsum(
                "ktr,krc->tc", part[1:], recv, preferred_element_type=jnp.float32
            )
        rounded = lax.reduce_precision(acc, exponent_bits=8, mantissa_bits=7)
        return short_filter(rounded, short_taps[:, s, :], tok_rows)

    last = order[-1]
    filtered = {s: project(s, relayed[s][1]) for s in order[:-1]}
    first = order[0]
    if relayed[last][1] is None:
        filtered[first], tied = lax.optimization_barrier((filtered[first], relayed[last][0]))
        relayed[last] = (tied, None)
    product = filtered[0] * filtered[2]
    blocks = tok_rows // block_rows
    current = product.reshape(blocks, block_rows, local_groups, group_size)
    near = jnp.einsum("gij,bjgc->bigc", kernel, current, precision=highest)
    ends = jnp.einsum("gni,bigc->bgnc", tail, current, precision=highest)
    step_decay = jnp.exp(-decay * block_rows)

    def advance(state, end_block):
        return (step_decay * state + end_block, state)

    zero_state = jnp.zeros((local_groups, mode_count, group_size), jnp.float32)
    own_state, local_starts = lax.scan(advance, zero_state, ends)
    incoming = jnp.zeros_like(own_state)
    for by in range(1, n_ctx):
        pairs = [(k, k + by) for k in range(n_ctx - by)]
        arrived = lax.ppermute(own_state, "ctx", pairs)
        incoming = incoming + jnp.exp(-decay * (tok_rows * (by - 1.0))) * arrived
    block_index = jnp.arange(blocks).astype(jnp.float32)
    lead = jnp.exp(-decay[None] * block_rows * block_index[:, None, None, None])
    starts = lead * incoming[None] + local_starts
    distant = jnp.einsum("gin,bgnc->bigc", entry, starts, precision=highest)
    conv_out = (near + distant).reshape(tok_rows, local_width)
    if relayed[last][1] is None:
        whole_w, conv_out = lax.optimization_barrier((relayed[last][0], conv_out))
        acc = jnp.dot(normed, whole_w, preferred_element_type=jnp.float32)
        rounded = lax.reduce_precision(acc, exponent_bits=8, mantissa_bits=7)
        second = short_filter(rounded, short_taps[:, last, :], tok_rows)
    else:
        late, conv_out = lax.optimization_barrier((relayed[last][1], conv_out))
        second = project(last, late)
    gated = (second * conv_out).astype(jnp.bfloat16)
    count = lax.axis_size("tp")
    me_tp = lax.axis_index("tp")

    def contribution(block, source):
        rows = lax.dynamic_slice_in_dim(w_out, source * local_width, local_width, axis=0)
        return jnp.dot(block, rows, preferred_element_type=jnp.float32)

    if count & (count - 1) == 0:
        mixed = contribution(gated, me_tp)
        held = gated[None]
        masks = [0]
        bit = count // 2
        while bit >= 1:
            pairs = [(q, q ^ bit) for q in range(count)]
            arrived = lax.ppermute(held, "tp", pairs)
            for q, m in enumerate(masks):
                mixed = mixed + contribution(arrived[q], jnp.bitwise_xor(me_tp, m ^ bit))
            held = jnp.concatenate([held, arrived], axis=0)
            masks = masks + [m ^ bit for m in masks]
            bit //= 2
    else:
        pieces = gather_by_swaps(gated, "tp")
        mixed = jnp.einsum("qtc,qcf->tf", pieces, w_out.reshape(pieces.shape[0], local_width, -1),
                           preferred_element_type=jnp.float32)
    return (tokens.astype(jnp.float32) + mixed).astype(jnp.bfloat16)


def solution(mesh):
    in_specs = (
        P(("grp", "ctx"), "tp"),
        P("tp"),
        P("ctx", None, "tp"),
        P(None, None, "tp"),
        P("tp", None),
        P("tp", None),
        P(None, "tp"),
    )
    out_specs = P(("grp", "ctx"), "tp")
    return jax.shard_map(body, mesh=mesh, in_specs=in_specs, out_specs=out_specs, check_vma=False)
```

```python
import jax
import jax.numpy as jnp
from jax import lax
from jax.sharding import PartitionSpec as P

BLOCK = 128


def shifted(x, axis, by):
    count = lax.axis_size(axis)
    pairs = [(i, i + by) for i in range(count) if 0 <= i + by < count]
    return lax.ppermute(x, axis, pairs)


def short_filter(extended, taps, count):
    values = extended.astype(jnp.float32)
    result = jnp.zeros((count, values.shape[1]), jnp.float32)
    span = taps.shape[0]
    for tap_index in range(span):
        begin = span - 1 - tap_index
        result = result + taps[tap_index] * values[begin : begin + count]
    return result


def banded(series):
    group_count, length = series.shape
    padded = jnp.concatenate([series, jnp.zeros_like(series)], axis=1)
    tiled = jnp.tile(padded, (1, length))
    return tiled[:, : length * (2 * length - 1)].reshape(group_count, length, 2 * length - 1)


def gather_by_permutes(x, axis):
    count = lax.axis_size(axis)
    me = lax.axis_index(axis)
    pieces = [x]
    for by in range(1, count):
        pairs = [(s, (s + by) % count) for s in range(count)]
        pieces.append(lax.ppermute(x, axis, pairs))
    stacked = jnp.stack(pieces[::-1], axis=0)
    return jnp.roll(stacked, me + 1, axis=0)


def gather_by_swaps(x, axis):
    count = lax.axis_size(axis)
    me = lax.axis_index(axis)
    bits = []
    b = 1
    while b < count:
        bits.append(b)
        b *= 2
    if 2 ** len(bits) != count:
        return lax.all_gather(x, axis, axis=0)
    held = x[None]
    masks = [0]
    for bit in bits[::-1]:
        pairs = [(q, q ^ bit) for q in range(count)]
        held = jnp.concatenate([held, lax.ppermute(held, axis, pairs)], axis=0)
        masks = masks + [m ^ bit for m in masks]
    inverse = [masks.index(m) for m in range(count)]
    table = jnp.array(inverse, jnp.int32)
    where = jnp.take(table, jnp.bitwise_xor(jnp.arange(count, dtype=jnp.int32), me))
    return jnp.take(held, where, axis=0)


def body(tokens, norm_gain, w_in, short_taps, rates, residues, w_out):
    tok_rows = tokens.shape[0]
    local_width = w_in.shape[2]
    local_groups = rates.shape[0]
    group_size = local_width // local_groups
    block_rows = BLOCK
    reach = block_rows - 1
    mode_count = rates.shape[1]
    highest = lax.Precision.HIGHEST
    n_ctx = lax.axis_size("ctx")
    n_grp = lax.axis_size("grp")
    me_ctx = lax.axis_index("ctx")
    me_grp = lax.axis_index("grp")
    shard_rows = w_in.shape[0]
    piece = shard_rows // n_grp
    streams = w_in.shape[1]

    span = short_taps.shape[0]
    halo = span - 1
    decay = rates[:, :, None]
    coef = residues * jnp.sqrt(-jnp.expm1(-2.0 * rates)) * mode_count ** (-0.5)
    lags = jnp.arange(block_rows).astype(jnp.float32)
    powers = jnp.exp(-decay * lags)
    long_taps = jnp.einsum("gn,gnt->gt", coef, powers, precision=highest)
    falling = coef[:, None, :] * jnp.exp(-rates[:, None, :] * lags[None, :, None])
    rising = jnp.exp(rates[:, None, :] * lags[None, :, None])
    square = jnp.einsum("gin,gjn->gij", falling, rising, precision=highest)
    kernel = jnp.where(lags[None, :, None] >= lags[None, None, :], square, 0.0)
    tail = jnp.exp(-decay * (reach - lags))
    entry = coef[:, None, :] * jnp.exp(-rates[:, None, :] * (lags[None, :, None] + 1.0))

    with_gain = jnp.concatenate([tokens, norm_gain[None]], axis=0)
    stacked = gather_by_swaps(with_gain, "tp")
    whole_rows = jnp.concatenate(list(stacked), axis=1)
    before = shifted(whole_rows[tok_rows - halo : tok_rows], "ctx", 1)
    gathered = jnp.concatenate([before, whole_rows], axis=0)
    own = lax.dynamic_slice_in_dim(w_in, me_grp * piece, piece, axis=0)

    def relay_send(got):
        doubled = jnp.concatenate([got, got], axis=0)
        return lax.dynamic_slice_in_dim(doubled, me_ctx + 1, n_ctx - 1, axis=0)

    def relay(send):
        received = []
        for by in range(1, n_grp):
            pairs = [(q, (q + by) % n_grp) for q in range(n_grp)]
            received.append(lax.ppermute(send, "grp", pairs))
        return received

    order = [0, 2, 1] if streams == 3 else list(range(streams))
    relayed = {}
    for s in order:
        got = lax.all_gather(own[:, s, :], "ctx", axis=0)
        if s == order[0]:
            got, kernel, tail, entry = lax.optimization_barrier((got, kernel, tail, entry))
        if s == order[-1] and len(order) > 1:
            relayed[s] = (got, None)
            continue
        send = relay_send(got)
        if s == order[0]:
            send, gathered = lax.optimization_barrier((send, gathered))
        relayed[s] = (got, relay(send))

    ext_rows = tok_rows + halo
    values = gathered[:ext_rows].astype(jnp.float32)
    gain_whole = gathered[ext_rows]
    scale = lax.rsqrt(jnp.mean(values * values, axis=1, keepdims=True) + 1e-06)
    normed = (values * scale * gain_whole.astype(jnp.float32)).astype(jnp.bfloat16)
    blocks = normed.reshape(ext_rows, n_ctx * n_grp, piece).transpose(1, 0, 2)
    shard_ids = jnp.arange(n_ctx, dtype=jnp.int32)
    mine = jnp.take(blocks, shard_ids * n_grp + me_grp, axis=0)
    others = []
    for by in range(1, n_grp):
        src_grp = (me_grp - by) % n_grp
        rolled = ((shard_ids + me_ctx) % n_ctx) * n_grp + src_grp
        others.append((src_grp, jnp.take(blocks, rolled, axis=0)))
    def project(s, received):
        got = relayed[s][0]
        acc = jnp.einsum("ktr,krc->tc", mine, got, preferred_element_type=jnp.float32)
        for (src_grp, part), recv in zip(others, received):
            local = lax.dynamic_slice_in_dim(w_in[:, s, :], src_grp * piece, piece, axis=0)
            acc = acc + jnp.dot(part[0], local, preferred_element_type=jnp.float32)
            acc = acc + jnp.einsum(
                "ktr,krc->tc", part[1:], recv, preferred_element_type=jnp.float32
            )
        rounded = lax.reduce_precision(acc, exponent_bits=8, mantissa_bits=7)
        return short_filter(rounded, short_taps[:, s, :], tok_rows)

    last = order[-1]
    filtered = {s: project(s, relayed[s][1]) for s in order[:-1]}
    first = order[0]
    if relayed[last][1] is None:
        early = [s for s in order[:-1]]
        held, tied = lax.optimization_barrier(([filtered[s] for s in early], relayed[last][0]))
        for s, value in zip(early, held):
            filtered[s] = value
        relayed[last] = (tied, relay(relay_send(tied)))
    product = filtered[0] * filtered[2]
    blocks = tok_rows // block_rows
    current = product.reshape(blocks, block_rows, local_groups, group_size)
    near = jnp.einsum("gij,bjgc->bigc", kernel, current, precision=highest)
    ends = jnp.einsum("gni,bigc->bgnc", tail, current, precision=highest)
    step_decay = jnp.exp(-decay * block_rows)

    def advance(state, end_block):
        return (step_decay * state + end_block, state)

    zero_state = jnp.zeros((local_groups, mode_count, group_size), jnp.float32)
    own_state, local_starts = lax.scan(advance, zero_state, ends)
    incoming = jnp.zeros_like(own_state)
    for by in range(1, n_ctx):
        pairs = [(k, k + by) for k in range(n_ctx - by)]
        arrived = lax.ppermute(own_state, "ctx", pairs)
        incoming = incoming + jnp.exp(-decay * (tok_rows * (by - 1.0))) * arrived
    block_index = jnp.arange(blocks).astype(jnp.float32)
    lead = jnp.exp(-decay[None] * block_rows * block_index[:, None, None, None])
    starts = lead * incoming[None] + local_starts
    distant = jnp.einsum("gin,bgnc->bigc", entry, starts, precision=highest)
    conv_out = (near + distant).reshape(tok_rows, local_width)
    late, conv_out = lax.optimization_barrier((relayed[last][1], conv_out))
    second = project(last, late)
    gated = (second * conv_out).astype(jnp.bfloat16)
    count = lax.axis_size("tp")
    me_tp = lax.axis_index("tp")

    def contribution(block, source):
        rows = lax.dynamic_slice_in_dim(w_out, source * local_width, local_width, axis=0)
        return jnp.dot(block, rows, preferred_element_type=jnp.float32)

    if count & (count - 1) == 0:
        mixed = contribution(gated, me_tp)
        held = gated[None]
        masks = [0]
        bit = count // 2
        while bit >= 1:
            pairs = [(q, q ^ bit) for q in range(count)]
            arrived = lax.ppermute(held, "tp", pairs)
            for q, m in enumerate(masks):
                mixed = mixed + contribution(arrived[q], jnp.bitwise_xor(me_tp, m ^ bit))
            held = jnp.concatenate([held, arrived], axis=0)
            masks = masks + [m ^ bit for m in masks]
            bit //= 2
    else:
        pieces = gather_by_swaps(gated, "tp")
        mixed = jnp.einsum("qtc,qcf->tf", pieces, w_out.reshape(pieces.shape[0], local_width, -1),
                           preferred_element_type=jnp.float32)
    return (tokens.astype(jnp.float32) + mixed).astype(jnp.bfloat16)


def solution(mesh):
    in_specs = (
        P(("grp", "ctx"), "tp"),
        P("tp"),
        P("ctx", None, "tp"),
        P(None, None, "tp"),
        P("tp", None),
        P("tp", None),
        P(None, "tp"),
    )
    out_specs = P(("grp", "ctx"), "tp")
    return jax.shard_map(body, mesh=mesh, in_specs=in_specs, out_specs=out_specs, check_vma=False)
```

```python
import jax
import jax.numpy as jnp
from jax import lax
from jax.sharding import PartitionSpec as P

BLOCK = 128


def shifted(x, axis, by):
    count = lax.axis_size(axis)
    pairs = [(i, i + by) for i in range(count) if 0 <= i + by < count]
    return lax.ppermute(x, axis, pairs)


def short_filter(extended, taps, count):
    values = extended.astype(jnp.float32)
    result = jnp.zeros((count, values.shape[1]), jnp.float32)
    span = taps.shape[0]
    for tap_index in range(span):
        begin = span - 1 - tap_index
        result = result + taps[tap_index] * values[begin : begin + count]
    return result


def banded(series):
    group_count, length = series.shape
    padded = jnp.concatenate([series, jnp.zeros_like(series)], axis=1)
    tiled = jnp.tile(padded, (1, length))
    return tiled[:, : length * (2 * length - 1)].reshape(group_count, length, 2 * length - 1)


def gather_by_permutes(x, axis):
    count = lax.axis_size(axis)
    me = lax.axis_index(axis)
    pieces = [x]
    for by in range(1, count):
        pairs = [(s, (s + by) % count) for s in range(count)]
        pieces.append(lax.ppermute(x, axis, pairs))
    stacked = jnp.stack(pieces[::-1], axis=0)
    return jnp.roll(stacked, me + 1, axis=0)


def gather_by_swaps(x, axis):
    count = lax.axis_size(axis)
    me = lax.axis_index(axis)
    bits = []
    b = 1
    while b < count:
        bits.append(b)
        b *= 2
    if 2 ** len(bits) != count:
        return lax.all_gather(x, axis, axis=0)
    held = x[None]
    masks = [0]
    for bit in bits[::-1]:
        pairs = [(q, q ^ bit) for q in range(count)]
        held = jnp.concatenate([held, lax.ppermute(held, axis, pairs)], axis=0)
        masks = masks + [m ^ bit for m in masks]
    inverse = [masks.index(m) for m in range(count)]
    table = jnp.array(inverse, jnp.int32)
    where = jnp.take(table, jnp.bitwise_xor(jnp.arange(count, dtype=jnp.int32), me))
    return jnp.take(held, where, axis=0)


def body(tokens, norm_gain, w_in, short_taps, rates, residues, w_out):
    tok_rows = tokens.shape[0]
    local_width = w_in.shape[2]
    local_groups = rates.shape[0]
    group_size = local_width // local_groups
    block_rows = BLOCK
    reach = block_rows - 1
    mode_count = rates.shape[1]
    highest = lax.Precision.HIGHEST
    n_ctx = lax.axis_size("ctx")
    n_grp = lax.axis_size("grp")
    me_ctx = lax.axis_index("ctx")
    me_grp = lax.axis_index("grp")
    shard_rows = w_in.shape[0]
    piece = shard_rows // n_grp
    streams = w_in.shape[1]

    span = short_taps.shape[0]
    halo = span - 1
    decay = rates[:, :, None]
    coef = residues * jnp.sqrt(-jnp.expm1(-2.0 * rates)) * mode_count ** (-0.5)
    lags = jnp.arange(block_rows).astype(jnp.float32)
    powers = jnp.exp(-decay * lags)
    long_taps = jnp.einsum("gn,gnt->gt", coef, powers, precision=highest)
    falling = coef[:, None, :] * jnp.exp(-rates[:, None, :] * lags[None, :, None])
    rising = jnp.exp(rates[:, None, :] * lags[None, :, None])
    square = jnp.einsum("gin,gjn->gij", falling, rising, precision=highest)
    kernel = jnp.where(lags[None, :, None] >= lags[None, None, :], square, 0.0)
    tail = jnp.exp(-decay * (reach - lags))
    entry = coef[:, None, :] * jnp.exp(-rates[:, None, :] * (lags[None, :, None] + 1.0))

    with_gain = jnp.concatenate([tokens, norm_gain[None]], axis=0)
    stacked = gather_by_swaps(with_gain, "tp")
    whole_rows = jnp.concatenate(list(stacked), axis=1)
    before = shifted(whole_rows[tok_rows - halo : tok_rows], "ctx", 1)
    gathered = jnp.concatenate([before, whole_rows], axis=0)
    own = lax.dynamic_slice_in_dim(w_in, me_grp * piece, piece, axis=0)

    def relay_send(got):
        doubled = jnp.concatenate([got, got], axis=0)
        return lax.dynamic_slice_in_dim(doubled, me_ctx + 1, n_ctx - 1, axis=0)

    def relay(send):
        received = []
        for by in range(1, n_grp):
            pairs = [(q, (q + by) % n_grp) for q in range(n_grp)]
            received.append(lax.ppermute(send, "grp", pairs))
        return received

    order = [0, 2, 1] if streams == 3 else list(range(streams))
    relayed = {}
    for s in order:
        got = lax.all_gather(own[:, s, :], "ctx", axis=0)
        if s == order[0]:
            got, kernel, tail, entry = lax.optimization_barrier((got, kernel, tail, entry))
        if s == order[-1] and len(order) > 1:
            relayed[s] = (got, None)
            continue
        send = relay_send(got)
        if s == order[0]:
            send, gathered = lax.optimization_barrier((send, gathered))
        relayed[s] = (got, relay(send))

    ext_rows = tok_rows + halo
    values = gathered[:ext_rows].astype(jnp.float32)
    gain_whole = gathered[ext_rows]
    scale = lax.rsqrt(jnp.mean(values * values, axis=1, keepdims=True) + 1e-06)
    normed = (values * scale * gain_whole.astype(jnp.float32)).astype(jnp.bfloat16)
    blocks = normed.reshape(ext_rows, n_ctx * n_grp, piece).transpose(1, 0, 2)
    shard_ids = jnp.arange(n_ctx, dtype=jnp.int32)
    mine = jnp.take(blocks, shard_ids * n_grp + me_grp, axis=0)
    others = []
    for by in range(1, n_grp):
        src_grp = (me_grp - by) % n_grp
        rolled = ((shard_ids + me_ctx) % n_ctx) * n_grp + src_grp
        others.append((src_grp, jnp.take(blocks, rolled, axis=0)))
    def project(s, received):
        got = relayed[s][0]
        acc = jnp.einsum("ktr,krc->tc", mine, got, preferred_element_type=jnp.float32)
        for (src_grp, part), recv in zip(others, received):
            local = lax.dynamic_slice_in_dim(w_in[:, s, :], src_grp * piece, piece, axis=0)
            acc = acc + jnp.dot(part[0], local, preferred_element_type=jnp.float32)
            acc = acc + jnp.einsum(
                "ktr,krc->tc", part[1:], recv, preferred_element_type=jnp.float32
            )
        rounded = lax.reduce_precision(acc, exponent_bits=8, mantissa_bits=7)
        return short_filter(rounded, short_taps[:, s, :], tok_rows)

    last = order[-1]
    filtered = {s: project(s, relayed[s][1]) for s in order[:-1]}
    first = order[0]
    count_is_pow2 = lax.axis_size("tp") & (lax.axis_size("tp") - 1) == 0
    if relayed[last][1] is None:
        early = [s for s in order[:-1]]
        held, tied = lax.optimization_barrier(([filtered[s] for s in early], relayed[last][0]))
        for s, value in zip(early, held):
            filtered[s] = value
        send = relay_send(tied)
        if local_width % 256 == 0 and count_is_pow2:
            cut = local_width // 2
            relayed[last] = (tied, (relay(send[..., :cut]), relay(send[..., cut:])))
        else:
            relayed[last] = (tied, relay(send))
    product = filtered[0] * filtered[2]
    blocks = tok_rows // block_rows
    current = product.reshape(blocks, block_rows, local_groups, group_size)
    near = jnp.einsum("gij,bjgc->bigc", kernel, current, precision=highest)
    ends = jnp.einsum("gni,bigc->bgnc", tail, current, precision=highest)
    step_decay = jnp.exp(-decay * block_rows)

    def advance(state, end_block):
        return (step_decay * state + end_block, state)

    zero_state = jnp.zeros((local_groups, mode_count, group_size), jnp.float32)
    own_state, local_starts = lax.scan(advance, zero_state, ends)
    incoming = jnp.zeros_like(own_state)
    for by in range(1, n_ctx):
        pairs = [(k, k + by) for k in range(n_ctx - by)]
        arrived = lax.ppermute(own_state, "ctx", pairs)
        incoming = incoming + jnp.exp(-decay * (tok_rows * (by - 1.0))) * arrived
    block_index = jnp.arange(blocks).astype(jnp.float32)
    lead = jnp.exp(-decay[None] * block_rows * block_index[:, None, None, None])
    starts = lead * incoming[None] + local_starts
    distant = jnp.einsum("gin,bgnc->bigc", entry, starts, precision=highest)
    conv_out = (near + distant).reshape(tok_rows, local_width)
    count = lax.axis_size("tp")
    me_tp = lax.axis_index("tp")

    def project_cols(received, lo, hi):
        got = relayed[last][0][..., lo:hi]
        acc = jnp.einsum("ktr,krc->tc", mine, got, preferred_element_type=jnp.float32)
        for (src_grp, part), recv in zip(others, received):
            local = lax.dynamic_slice_in_dim(w_in[:, last, lo:hi], src_grp * piece, piece, axis=0)
            acc = acc + jnp.dot(part[0], local, preferred_element_type=jnp.float32)
            acc = acc + jnp.einsum(
                "ktr,krc->tc", part[1:], recv, preferred_element_type=jnp.float32
            )
        rounded = lax.reduce_precision(acc, exponent_bits=8, mantissa_bits=7)
        return short_filter(rounded, short_taps[:, last, lo:hi], tok_rows)

    def contribution(block, source, lo):
        width = block.shape[1]
        rows = lax.dynamic_slice_in_dim(w_out, source * local_width + lo, width, axis=0)
        return jnp.dot(block, rows, preferred_element_type=jnp.float32)

    def swap_project(gated_part, lo):
        mixed = contribution(gated_part, me_tp, lo)
        held = gated_part[None]
        masks = [0]
        bit = count // 2
        while bit >= 1:
            pairs = [(q, q ^ bit) for q in range(count)]
            arrived = lax.ppermute(held, "tp", pairs)
            for q, m in enumerate(masks):
                mixed = mixed + contribution(arrived[q], jnp.bitwise_xor(me_tp, m ^ bit), lo)
            held = jnp.concatenate([held, arrived], axis=0)
            masks = masks + [m ^ bit for m in masks]
            bit //= 2
        return mixed

    if isinstance(relayed[last][1], tuple):
        first_half, second_half = relayed[last][1]
        cut = local_width // 2
        late_a, conv_out = lax.optimization_barrier((first_half, conv_out))
        gated_a = (project_cols(late_a, 0, cut) * conv_out[:, :cut]).astype(jnp.bfloat16)
        late_b, gated_a = lax.optimization_barrier((second_half, gated_a))
        gated_b = (project_cols(late_b, cut, local_width) * conv_out[:, cut:]).astype(jnp.bfloat16)
        mixed = swap_project(gated_a, 0) + swap_project(gated_b, cut)
    else:
        late, conv_out = lax.optimization_barrier((relayed[last][1], conv_out))
        second = project(last, late)
        gated = (second * conv_out).astype(jnp.bfloat16)
        if count_is_pow2:
            mixed = swap_project(gated, 0)
        else:
            pieces = gather_by_swaps(gated, "tp")
            mixed = jnp.einsum("qtc,qcf->tf", pieces, w_out.reshape(pieces.shape[0], local_width, -1),
                               preferred_element_type=jnp.float32)
    return (tokens.astype(jnp.float32) + mixed).astype(jnp.bfloat16)


def solution(mesh):
    in_specs = (
        P(("grp", "ctx"), "tp"),
        P("tp"),
        P("ctx", None, "tp"),
        P(None, None, "tp"),
        P("tp", None),
        P("tp", None),
        P(None, "tp"),
    )
    out_specs = P(("grp", "ctx"), "tp")
    return jax.shard_map(body, mesh=mesh, in_specs=in_specs, out_specs=out_specs, check_vma=False)
```

```python
import jax
import jax.numpy as jnp
from jax import lax
from jax.sharding import PartitionSpec as P

BLOCK = 128


def shifted(x, axis, by):
    count = lax.axis_size(axis)
    pairs = [(i, i + by) for i in range(count) if 0 <= i + by < count]
    return lax.ppermute(x, axis, pairs)


def short_filter(extended, taps, count):
    values = extended.astype(jnp.float32)
    result = jnp.zeros((count, values.shape[1]), jnp.float32)
    span = taps.shape[0]
    for tap_index in range(span):
        begin = span - 1 - tap_index
        result = result + taps[tap_index] * values[begin : begin + count]
    return result


def banded(series):
    group_count, length = series.shape
    padded = jnp.concatenate([series, jnp.zeros_like(series)], axis=1)
    tiled = jnp.tile(padded, (1, length))
    return tiled[:, : length * (2 * length - 1)].reshape(group_count, length, 2 * length - 1)


def gather_by_permutes(x, axis):
    count = lax.axis_size(axis)
    me = lax.axis_index(axis)
    pieces = [x]
    for by in range(1, count):
        pairs = [(s, (s + by) % count) for s in range(count)]
        pieces.append(lax.ppermute(x, axis, pairs))
    stacked = jnp.stack(pieces[::-1], axis=0)
    return jnp.roll(stacked, me + 1, axis=0)


def gather_by_swaps(x, axis):
    count = lax.axis_size(axis)
    me = lax.axis_index(axis)
    bits = []
    b = 1
    while b < count:
        bits.append(b)
        b *= 2
    if 2 ** len(bits) != count:
        return lax.all_gather(x, axis, axis=0)
    held = x[None]
    masks = [0]
    for bit in bits[::-1]:
        pairs = [(q, q ^ bit) for q in range(count)]
        held = jnp.concatenate([held, lax.ppermute(held, axis, pairs)], axis=0)
        masks = masks + [m ^ bit for m in masks]
    inverse = [masks.index(m) for m in range(count)]
    table = jnp.array(inverse, jnp.int32)
    where = jnp.take(table, jnp.bitwise_xor(jnp.arange(count, dtype=jnp.int32), me))
    return jnp.take(held, where, axis=0)


def body(tokens, norm_gain, w_in, short_taps, rates, residues, w_out):
    tok_rows = tokens.shape[0]
    local_width = w_in.shape[2]
    local_groups = rates.shape[0]
    group_size = local_width // local_groups
    block_rows = BLOCK
    reach = block_rows - 1
    mode_count = rates.shape[1]
    highest = lax.Precision.HIGHEST
    n_ctx = lax.axis_size("ctx")
    n_grp = lax.axis_size("grp")
    me_ctx = lax.axis_index("ctx")
    me_grp = lax.axis_index("grp")
    shard_rows = w_in.shape[0]
    piece = shard_rows // n_grp
    streams = w_in.shape[1]

    span = short_taps.shape[0]
    halo = span - 1
    decay = rates[:, :, None]
    coef = residues * jnp.sqrt(-jnp.expm1(-2.0 * rates)) * mode_count ** (-0.5)
    lags = jnp.arange(block_rows).astype(jnp.float32)
    powers = jnp.exp(-decay * lags)
    long_taps = jnp.einsum("gn,gnt->gt", coef, powers, precision=highest)
    falling = coef[:, None, :] * jnp.exp(-rates[:, None, :] * lags[None, :, None])
    rising = jnp.exp(rates[:, None, :] * lags[None, :, None])
    square = jnp.einsum("gin,gjn->gij", falling, rising, precision=highest)
    kernel = jnp.where(lags[None, :, None] >= lags[None, None, :], square, 0.0)
    tail = jnp.exp(-decay * (reach - lags))
    entry = coef[:, None, :] * jnp.exp(-rates[:, None, :] * (lags[None, :, None] + 1.0))

    with_gain = jnp.concatenate([tokens, norm_gain[None]], axis=0)
    stacked = gather_by_swaps(with_gain, "tp")
    whole_rows = jnp.concatenate(list(stacked), axis=1)
    before = shifted(whole_rows[tok_rows - halo : tok_rows], "ctx", 1)
    gathered = jnp.concatenate([before, whole_rows], axis=0)
    own = lax.dynamic_slice_in_dim(w_in, me_grp * piece, piece, axis=0)

    def relay_send(got):
        picks = (me_ctx + 1 + jnp.arange(n_ctx - 1, dtype=jnp.int32)) % n_ctx
        return jnp.take(got, picks, axis=0)

    def relay(send):
        received = []
        for by in range(1, n_grp):
            pairs = [(q, (q + by) % n_grp) for q in range(n_grp)]
            received.append(lax.ppermute(send, "grp", pairs))
        return received

    order = [0, 2, 1] if streams == 3 else list(range(streams))
    relayed = {}
    for s in order:
        got = lax.all_gather(own[:, s, :], "ctx", axis=0)
        if s == order[0]:
            got, kernel, tail, entry = lax.optimization_barrier((got, kernel, tail, entry))
        if s == order[-1] and len(order) > 1:
            relayed[s] = (got, None)
            continue
        send = relay_send(got)
        if s == order[0]:
            send, gathered = lax.optimization_barrier((send, gathered))
        relayed[s] = (got, relay(send))

    ext_rows = tok_rows + halo
    values = gathered[:ext_rows].astype(jnp.float32)
    gain_whole = gathered[ext_rows]
    scale = lax.rsqrt(jnp.mean(values * values, axis=1, keepdims=True) + 1e-06)
    normed = (values * scale * gain_whole.astype(jnp.float32)).astype(jnp.bfloat16)
    blocks = normed.reshape(ext_rows, n_ctx * n_grp, piece).transpose(1, 0, 2)
    shard_ids = jnp.arange(n_ctx, dtype=jnp.int32)
    mine = jnp.take(blocks, shard_ids * n_grp + me_grp, axis=0)
    others = []
    for by in range(1, n_grp):
        src_grp = (me_grp - by) % n_grp
        rolled = ((shard_ids + me_ctx) % n_ctx) * n_grp + src_grp
        others.append((src_grp, jnp.take(blocks, rolled, axis=0)))
    def project(s, received):
        got = relayed[s][0]
        acc = jnp.einsum("ktr,krc->tc", mine, got, preferred_element_type=jnp.float32)
        for (src_grp, part), recv in zip(others, received):
            local = lax.dynamic_slice_in_dim(w_in[:, s, :], src_grp * piece, piece, axis=0)
            acc = acc + jnp.dot(part[0], local, preferred_element_type=jnp.float32)
            acc = acc + jnp.einsum(
                "ktr,krc->tc", part[1:], recv, preferred_element_type=jnp.float32
            )
        rounded = lax.reduce_precision(acc, exponent_bits=8, mantissa_bits=7)
        return short_filter(rounded, short_taps[:, s, :], tok_rows)

    last = order[-1]
    filtered = {s: project(s, relayed[s][1]) for s in order[:-1]}
    first = order[0]
    if relayed[last][1] is None:
        early = [s for s in order[:-1]]
        held, tied = lax.optimization_barrier(([filtered[s] for s in early], relayed[last][0]))
        for s, value in zip(early, held):
            filtered[s] = value
        relayed[last] = (tied, relay(relay_send(tied)))
    product = filtered[0] * filtered[2]
    blocks = tok_rows // block_rows
    current = product.reshape(blocks, block_rows, local_groups, group_size)
    near = jnp.einsum("gij,bjgc->bigc", kernel, current, precision=highest)
    ends = jnp.einsum("gni,bigc->bgnc", tail, current, precision=highest)
    step_decay = jnp.exp(-decay * block_rows)

    def advance(state, end_block):
        return (step_decay * state + end_block, state)

    zero_state = jnp.zeros((local_groups, mode_count, group_size), jnp.float32)
    own_state, local_starts = lax.scan(advance, zero_state, ends)
    incoming = jnp.zeros_like(own_state)
    for by in range(1, n_ctx):
        pairs = [(k, k + by) for k in range(n_ctx - by)]
        arrived = lax.ppermute(own_state, "ctx", pairs)
        incoming = incoming + jnp.exp(-decay * (tok_rows * (by - 1.0))) * arrived
    block_index = jnp.arange(blocks).astype(jnp.float32)
    lead = jnp.exp(-decay[None] * block_rows * block_index[:, None, None, None])
    starts = lead * incoming[None] + local_starts
    distant = jnp.einsum("gin,bgnc->bigc", entry, starts, precision=highest)
    conv_out = (near + distant).reshape(tok_rows, local_width)
    late, conv_out = lax.optimization_barrier((relayed[last][1], conv_out))
    second = project(last, late)
    gated = (second * conv_out).astype(jnp.bfloat16)
    count = lax.axis_size("tp")
    me_tp = lax.axis_index("tp")

    def contribution(block, source):
        rows = lax.dynamic_slice_in_dim(w_out, source * local_width, local_width, axis=0)
        return jnp.dot(block, rows, preferred_element_type=jnp.float32)

    if count & (count - 1) == 0:
        mixed = contribution(gated, me_tp)
        held = gated[None]
        masks = [0]
        bit = count // 2
        while bit >= 1:
            pairs = [(q, q ^ bit) for q in range(count)]
            arrived = lax.ppermute(held, "tp", pairs)
            for q, m in enumerate(masks):
                mixed = mixed + contribution(arrived[q], jnp.bitwise_xor(me_tp, m ^ bit))
            held = jnp.concatenate([held, arrived], axis=0)
            masks = masks + [m ^ bit for m in masks]
            bit //= 2
    else:
        pieces = gather_by_swaps(gated, "tp")
        mixed = jnp.einsum("qtc,qcf->tf", pieces, w_out.reshape(pieces.shape[0], local_width, -1),
                           preferred_element_type=jnp.float32)
    return (tokens.astype(jnp.float32) + mixed).astype(jnp.bfloat16)


def solution(mesh):
    in_specs = (
        P(("grp", "ctx"), "tp"),
        P("tp"),
        P("ctx", None, "tp"),
        P(None, None, "tp"),
        P("tp", None),
        P("tp", None),
        P(None, "tp"),
    )
    out_specs = P(("grp", "ctx"), "tp")
    return jax.shard_map(body, mesh=mesh, in_specs=in_specs, out_specs=out_specs, check_vma=False)
```

```python
import jax
import jax.numpy as jnp
from jax import lax
from jax.sharding import PartitionSpec as P

BLOCK = 128


def shifted(x, axis, by):
    count = lax.axis_size(axis)
    pairs = [(i, i + by) for i in range(count) if 0 <= i + by < count]
    return lax.ppermute(x, axis, pairs)


def short_filter(extended, taps, count):
    values = extended.astype(jnp.float32)
    result = jnp.zeros((count, values.shape[1]), jnp.float32)
    span = taps.shape[0]
    for tap_index in range(span):
        begin = span - 1 - tap_index
        result = result + taps[tap_index] * values[begin : begin + count]
    return result


def banded(series):
    group_count, length = series.shape
    padded = jnp.concatenate([series, jnp.zeros_like(series)], axis=1)
    tiled = jnp.tile(padded, (1, length))
    return tiled[:, : length * (2 * length - 1)].reshape(group_count, length, 2 * length - 1)


def gather_by_permutes(x, axis):
    count = lax.axis_size(axis)
    me = lax.axis_index(axis)
    pieces = [x]
    for by in range(1, count):
        pairs = [(s, (s + by) % count) for s in range(count)]
        pieces.append(lax.ppermute(x, axis, pairs))
    stacked = jnp.stack(pieces[::-1], axis=0)
    return jnp.roll(stacked, me + 1, axis=0)


def gather_by_swaps(x, axis):
    count = lax.axis_size(axis)
    me = lax.axis_index(axis)
    bits = []
    b = 1
    while b < count:
        bits.append(b)
        b *= 2
    if 2 ** len(bits) != count:
        return lax.all_gather(x, axis, axis=0)
    held = x[None]
    masks = [0]
    for bit in bits[::-1]:
        pairs = [(q, q ^ bit) for q in range(count)]
        held = jnp.concatenate([held, lax.ppermute(held, axis, pairs)], axis=0)
        masks = masks + [m ^ bit for m in masks]
    inverse = [masks.index(m) for m in range(count)]
    table = jnp.array(inverse, jnp.int32)
    where = jnp.take(table, jnp.bitwise_xor(jnp.arange(count, dtype=jnp.int32), me))
    return jnp.take(held, where, axis=0)


def body(tokens, norm_gain, w_in, short_taps, rates, residues, w_out):
    tok_rows = tokens.shape[0]
    local_width = w_in.shape[2]
    local_groups = rates.shape[0]
    group_size = local_width // local_groups
    block_rows = BLOCK
    reach = block_rows - 1
    mode_count = rates.shape[1]
    highest = lax.Precision.HIGHEST
    n_ctx = lax.axis_size("ctx")
    n_grp = lax.axis_size("grp")
    me_ctx = lax.axis_index("ctx")
    me_grp = lax.axis_index("grp")
    shard_rows = w_in.shape[0]
    piece = shard_rows // n_grp
    streams = w_in.shape[1]

    span = short_taps.shape[0]
    halo = span - 1
    decay = rates[:, :, None]
    coef = residues * jnp.sqrt(-jnp.expm1(-2.0 * rates)) * mode_count ** (-0.5)
    lags = jnp.arange(block_rows).astype(jnp.float32)
    powers = jnp.exp(-decay * lags)
    long_taps = jnp.einsum("gn,gnt->gt", coef, powers, precision=highest)
    falling = coef[:, None, :] * jnp.exp(-rates[:, None, :] * lags[None, :, None])
    rising = jnp.exp(rates[:, None, :] * lags[None, :, None])
    square = jnp.einsum("gin,gjn->gij", falling, rising, precision=highest)
    kernel = jnp.where(lags[None, :, None] >= lags[None, None, :], square, 0.0)
    tail = jnp.exp(-decay * (reach - lags))
    entry = coef[:, None, :] * jnp.exp(-rates[:, None, :] * (lags[None, :, None] + 1.0))

    with_gain = jnp.concatenate([tokens, norm_gain[None]], axis=0)
    stacked = gather_by_swaps(with_gain, "tp")
    whole_rows = jnp.concatenate(list(stacked), axis=1)
    before = shifted(whole_rows[tok_rows - halo : tok_rows], "ctx", 1)
    gathered = jnp.concatenate([before, whole_rows], axis=0)
    own = lax.dynamic_slice_in_dim(w_in, me_grp * piece, piece, axis=0)

    def relay_send(got):
        doubled = jnp.concatenate([got, got], axis=0)
        return lax.dynamic_slice_in_dim(doubled, me_ctx + 1, n_ctx - 1, axis=0)

    def relay(send):
        received = []
        for by in range(1, n_grp):
            pairs = [(q, (q + by) % n_grp) for q in range(n_grp)]
            received.append(lax.ppermute(send, "grp", pairs))
        return received

    order = [0, 2, 1] if streams == 3 else list(range(streams))
    relayed = {}
    for s in order:
        got = lax.all_gather(own[:, s, :], "ctx", axis=0)
        if s == order[0]:
            got, kernel, tail, entry = lax.optimization_barrier((got, kernel, tail, entry))
        if s == order[-1] and len(order) > 1:
            relayed[s] = (got, None)
            continue
        send = relay_send(got)
        if s == order[0]:
            send, gathered = lax.optimization_barrier((send, gathered))
        relayed[s] = (got, relay(send))

    ext_rows = tok_rows + halo
    values = gathered[:ext_rows].astype(jnp.float32)
    gain_whole = gathered[ext_rows]
    scale = lax.rsqrt(jnp.mean(values * values, axis=1, keepdims=True) + 1e-06)
    normed = (values * scale * gain_whole.astype(jnp.float32)).astype(jnp.bfloat16)
    blocks = normed.reshape(ext_rows, n_ctx * n_grp, piece).transpose(1, 0, 2)
    shard_ids = jnp.arange(n_ctx, dtype=jnp.int32)
    mine = jnp.take(blocks, shard_ids * n_grp + me_grp, axis=0)
    others = []
    for by in range(1, n_grp):
        src_grp = (me_grp - by) % n_grp
        rolled = ((shard_ids + me_ctx) % n_ctx) * n_grp + src_grp
        others.append((src_grp, jnp.take(blocks, rolled, axis=0)))
    def project(s, received):
        got = relayed[s][0]
        acc = jnp.einsum("ktr,krc->tc", mine, got, preferred_element_type=jnp.float32)
        for (src_grp, part), recv in zip(others, received):
            local = lax.dynamic_slice_in_dim(w_in[:, s, :], src_grp * piece, piece, axis=0)
            acc = acc + jnp.dot(part[0], local, preferred_element_type=jnp.float32)
            acc = acc + jnp.einsum(
                "ktr,krc->tc", part[1:], recv, preferred_element_type=jnp.float32
            )
        rounded = lax.reduce_precision(acc, exponent_bits=8, mantissa_bits=7)
        return short_filter(rounded, short_taps[:, s, :], tok_rows)

    last = order[-1]
    filtered = {s: project(s, relayed[s][1]) for s in order[:-1]}
    first = order[0]
    if relayed[last][1] is None:
        early = [s for s in order[:-1]]
        held, tied = lax.optimization_barrier(([filtered[s] for s in early], relayed[last][0]))
        for s, value in zip(early, held):
            filtered[s] = value
        relayed[last] = (tied, relay(relay_send(tied)))
    product = filtered[0] * filtered[2]
    blocks = tok_rows // block_rows
    current = product.reshape(blocks, block_rows, local_groups, group_size)
    near = jnp.einsum("gij,bjgc->bigc", kernel, current, precision=highest)
    ends = jnp.einsum("gni,bigc->bgnc", tail, current, precision=highest)
    step_decay = jnp.exp(-decay * block_rows)

    def advance(state, end_block):
        return (step_decay * state + end_block, state)

    zero_state = jnp.zeros((local_groups, mode_count, group_size), jnp.float32)
    own_state, local_starts = lax.scan(advance, zero_state, ends, unroll=True)
    incoming = jnp.zeros_like(own_state)
    for by in range(1, n_ctx):
        pairs = [(k, k + by) for k in range(n_ctx - by)]
        arrived = lax.ppermute(own_state, "ctx", pairs)
        incoming = incoming + jnp.exp(-decay * (tok_rows * (by - 1.0))) * arrived
    block_index = jnp.arange(blocks).astype(jnp.float32)
    lead = jnp.exp(-decay[None] * block_rows * block_index[:, None, None, None])
    starts = lead * incoming[None] + local_starts
    distant = jnp.einsum("gin,bgnc->bigc", entry, starts, precision=highest)
    conv_out = (near + distant).reshape(tok_rows, local_width)
    late, conv_out = lax.optimization_barrier((relayed[last][1], conv_out))
    second = project(last, late)
    gated = (second * conv_out).astype(jnp.bfloat16)
    count = lax.axis_size("tp")
    me_tp = lax.axis_index("tp")

    def contribution(block, source):
        rows = lax.dynamic_slice_in_dim(w_out, source * local_width, local_width, axis=0)
        return jnp.dot(block, rows, preferred_element_type=jnp.float32)

    if count & (count - 1) == 0:
        mixed = contribution(gated, me_tp)
        held = gated[None]
        masks = [0]
        bit = count // 2
        while bit >= 1:
            pairs = [(q, q ^ bit) for q in range(count)]
            arrived = lax.ppermute(held, "tp", pairs)
            for q, m in enumerate(masks):
                mixed = mixed + contribution(arrived[q], jnp.bitwise_xor(me_tp, m ^ bit))
            held = jnp.concatenate([held, arrived], axis=0)
            masks = masks + [m ^ bit for m in masks]
            bit //= 2
    else:
        pieces = gather_by_swaps(gated, "tp")
        mixed = jnp.einsum("qtc,qcf->tf", pieces, w_out.reshape(pieces.shape[0], local_width, -1),
                           preferred_element_type=jnp.float32)
    return (tokens.astype(jnp.float32) + mixed).astype(jnp.bfloat16)


def solution(mesh):
    in_specs = (
        P(("grp", "ctx"), "tp"),
        P("tp"),
        P("ctx", None, "tp"),
        P(None, None, "tp"),
        P("tp", None),
        P("tp", None),
        P(None, "tp"),
    )
    out_specs = P(("grp", "ctx"), "tp")
    return jax.shard_map(body, mesh=mesh, in_specs=in_specs, out_specs=out_specs, check_vma=False)
```

```python
import jax
import jax.numpy as jnp
from jax import lax
from jax.sharding import PartitionSpec as P

BLOCK = 128


def shifted(x, axis, by):
    count = lax.axis_size(axis)
    pairs = [(i, i + by) for i in range(count) if 0 <= i + by < count]
    return lax.ppermute(x, axis, pairs)


def short_filter(extended, taps, count):
    values = extended.astype(jnp.float32)
    result = jnp.zeros((count, values.shape[1]), jnp.float32)
    span = taps.shape[0]
    for tap_index in range(span):
        begin = span - 1 - tap_index
        result = result + taps[tap_index] * values[begin : begin + count]
    return result


def banded(series):
    group_count, length = series.shape
    padded = jnp.concatenate([series, jnp.zeros_like(series)], axis=1)
    tiled = jnp.tile(padded, (1, length))
    return tiled[:, : length * (2 * length - 1)].reshape(group_count, length, 2 * length - 1)


def gather_by_permutes(x, axis):
    count = lax.axis_size(axis)
    me = lax.axis_index(axis)
    pieces = [x]
    for by in range(1, count):
        pairs = [(s, (s + by) % count) for s in range(count)]
        pieces.append(lax.ppermute(x, axis, pairs))
    stacked = jnp.stack(pieces[::-1], axis=0)
    return jnp.roll(stacked, me + 1, axis=0)


def gather_by_swaps(x, axis):
    count = lax.axis_size(axis)
    me = lax.axis_index(axis)
    bits = []
    b = 1
    while b < count:
        bits.append(b)
        b *= 2
    if 2 ** len(bits) != count:
        return lax.all_gather(x, axis, axis=0)
    held = x[None]
    masks = [0]
    for bit in bits[::-1]:
        pairs = [(q, q ^ bit) for q in range(count)]
        held = jnp.concatenate([held, lax.ppermute(held, axis, pairs)], axis=0)
        masks = masks + [m ^ bit for m in masks]
    inverse = [masks.index(m) for m in range(count)]
    table = jnp.array(inverse, jnp.int32)
    where = jnp.take(table, jnp.bitwise_xor(jnp.arange(count, dtype=jnp.int32), me))
    return jnp.take(held, where, axis=0)


def body(tokens, norm_gain, w_in, short_taps, rates, residues, w_out):
    tok_rows = tokens.shape[0]
    local_width = w_in.shape[2]
    local_groups = rates.shape[0]
    group_size = local_width // local_groups
    block_rows = BLOCK
    reach = block_rows - 1
    mode_count = rates.shape[1]
    highest = lax.Precision.HIGHEST
    n_ctx = lax.axis_size("ctx")
    n_grp = lax.axis_size("grp")
    me_ctx = lax.axis_index("ctx")
    me_grp = lax.axis_index("grp")
    shard_rows = w_in.shape[0]
    piece = shard_rows // n_grp
    streams = w_in.shape[1]

    span = short_taps.shape[0]
    halo = span - 1
    decay = rates[:, :, None]
    coef = residues * jnp.sqrt(-jnp.expm1(-2.0 * rates)) * mode_count ** (-0.5)
    lags = jnp.arange(block_rows).astype(jnp.float32)
    powers = jnp.exp(-decay * lags)
    long_taps = jnp.einsum("gn,gnt->gt", coef, powers, precision=highest)
    falling = coef[:, None, :] * jnp.exp(-rates[:, None, :] * lags[None, :, None])
    rising = jnp.exp(rates[:, None, :] * lags[None, :, None])
    square = jnp.einsum("gin,gjn->gij", falling, rising, precision=highest)
    kernel = jnp.where(lags[None, :, None] >= lags[None, None, :], square, 0.0)
    tail = jnp.exp(-decay * (reach - lags))
    entry = coef[:, None, :] * jnp.exp(-rates[:, None, :] * (lags[None, :, None] + 1.0))

    with_gain = jnp.concatenate([tokens, norm_gain[None]], axis=0)
    stacked = gather_by_swaps(with_gain, "tp")
    whole_rows = jnp.concatenate(list(stacked), axis=1)
    before = shifted(whole_rows[tok_rows - halo : tok_rows], "ctx", 1)
    gathered = jnp.concatenate([before, whole_rows], axis=0)
    own = lax.dynamic_slice_in_dim(w_in, me_grp * piece, piece, axis=0)

    def relay_send(got):
        doubled = jnp.concatenate([got, got], axis=0)
        return lax.dynamic_slice_in_dim(doubled, me_ctx + 1, n_ctx - 1, axis=0)

    def relay(send):
        received = []
        for by in range(1, n_grp):
            pairs = [(q, (q + by) % n_grp) for q in range(n_grp)]
            received.append(lax.ppermute(send, "grp", pairs))
        return received

    order = [0, 2, 1] if streams == 3 else list(range(streams))
    relayed = {}
    for s in order:
        got = lax.all_gather(own[:, s, :], "ctx", axis=0)
        if s == order[0]:
            got, kernel, tail, entry = lax.optimization_barrier((got, kernel, tail, entry))
        if s == order[-1] and len(order) > 1:
            relayed[s] = (got, None)
            continue
        send = relay_send(got)
        if s == order[0]:
            send, gathered = lax.optimization_barrier((send, gathered))
        relayed[s] = (got, relay(send))

    ext_rows = tok_rows + halo
    values = gathered[:ext_rows].astype(jnp.float32)
    gain_whole = gathered[ext_rows]
    scale = lax.rsqrt(jnp.mean(values * values, axis=1, keepdims=True) + 1e-06)
    normed = (values * scale * gain_whole.astype(jnp.float32)).astype(jnp.bfloat16)
    blocks = normed.reshape(ext_rows, n_ctx * n_grp, piece).transpose(1, 0, 2)
    shard_ids = jnp.arange(n_ctx, dtype=jnp.int32)
    mine = jnp.take(blocks, shard_ids * n_grp + me_grp, axis=0)
    others = []
    for by in range(1, n_grp):
        src_grp = (me_grp - by) % n_grp
        rolled = ((shard_ids + me_ctx) % n_ctx) * n_grp + src_grp
        others.append((src_grp, jnp.take(blocks, rolled, axis=0)))
    def project(s, received):
        got = relayed[s][0]
        acc = jnp.einsum("ktr,krc->tc", mine, got, preferred_element_type=jnp.float32)
        for (src_grp, part), recv in zip(others, received):
            local = lax.dynamic_slice_in_dim(w_in[:, s, :], src_grp * piece, piece, axis=0)
            acc = acc + jnp.dot(part[0], local, preferred_element_type=jnp.float32)
            acc = acc + jnp.einsum(
                "ktr,krc->tc", part[1:], recv, preferred_element_type=jnp.float32
            )
        rounded = lax.reduce_precision(acc, exponent_bits=8, mantissa_bits=7)
        return short_filter(rounded, short_taps[:, s, :], tok_rows)

    last = order[-1]
    filtered = {s: project(s, relayed[s][1]) for s in order[:-1]}
    first = order[0]
    if relayed[last][1] is None:
        early = [s for s in order[:-1]]
        held, tied = lax.optimization_barrier(([filtered[s] for s in early], relayed[last][0]))
        for s, value in zip(early, held):
            filtered[s] = value
        relayed[last] = (tied, relay(relay_send(tied)))
    product = filtered[0] * filtered[2]
    blocks = tok_rows // block_rows
    current = product.reshape(blocks, block_rows, local_groups, group_size)
    near = jnp.einsum("gij,bjgc->bigc", kernel, current, precision=highest)
    ends = jnp.einsum("gni,bigc->bgnc", tail, current, precision=highest)
    step_decay = jnp.exp(-decay * block_rows)

    def advance(state, end_block):
        return (step_decay * state + end_block, state)

    zero_state = jnp.zeros((local_groups, mode_count, group_size), jnp.float32)
    own_state, local_starts = lax.scan(advance, zero_state, ends)
    incoming = jnp.zeros_like(own_state)
    for by in range(1, n_ctx):
        pairs = [(k, k + by) for k in range(n_ctx - by)]
        arrived = lax.ppermute(own_state, "ctx", pairs)
        incoming = incoming + jnp.exp(-decay * (tok_rows * (by - 1.0))) * arrived
    block_index = jnp.arange(blocks).astype(jnp.float32)
    lead = jnp.exp(-decay[None] * block_rows * block_index[:, None, None, None])
    starts = lead * incoming[None] + local_starts
    distant = jnp.einsum("gin,bgnc->bigc", entry, starts, precision=highest)
    conv_out = (near + distant).reshape(tok_rows, local_width)
    late, conv_out = lax.optimization_barrier((relayed[last][1], conv_out))
    second = project(last, late)
    gated = (second * conv_out).astype(jnp.bfloat16)
    count = lax.axis_size("tp")
    me_tp = lax.axis_index("tp")

    def contribution(block, source):
        rows = lax.dynamic_slice_in_dim(w_out, source * local_width, local_width, axis=0)
        return jnp.dot(block, rows, preferred_element_type=jnp.float32)

    if count & (count - 1) == 0:
        mixed = tokens.astype(jnp.float32) + contribution(gated, me_tp)
        held = gated[None]
        masks = [0]
        bit = count // 2
        while bit >= 1:
            pairs = [(q, q ^ bit) for q in range(count)]
            arrived = lax.ppermute(held, "tp", pairs)
            for q, m in enumerate(masks):
                mixed = mixed + contribution(arrived[q], jnp.bitwise_xor(me_tp, m ^ bit))
            held = jnp.concatenate([held, arrived], axis=0)
            masks = masks + [m ^ bit for m in masks]
            bit //= 2
        return mixed.astype(jnp.bfloat16)
    else:
        pieces = gather_by_swaps(gated, "tp")
        mixed = jnp.einsum("qtc,qcf->tf", pieces, w_out.reshape(pieces.shape[0], local_width, -1),
                           preferred_element_type=jnp.float32)
    return (tokens.astype(jnp.float32) + mixed).astype(jnp.bfloat16)


def solution(mesh):
    in_specs = (
        P(("grp", "ctx"), "tp"),
        P("tp"),
        P("ctx", None, "tp"),
        P(None, None, "tp"),
        P("tp", None),
        P("tp", None),
        P(None, "tp"),
    )
    out_specs = P(("grp", "ctx"), "tp")
    return jax.shard_map(body, mesh=mesh, in_specs=in_specs, out_specs=out_specs, check_vma=False)
```
